1024 devices in a mesh: dp: 32 (over y, x, core), expert: 32 (over z).
Axes of the slice: x: 4, y: 4, z: 32, core: 2. Of those that a mesh axis runs over, the one named last changes fastest.
Arguments:
- tokens: bfloat16 [1280, 4096], P('expert'), may hold values from -6 to 6
- cotangent: bfloat16 [1280, 4096], P('expert'), may hold values from -6 to 6
- expert_ids: int32 [1280, 8], P('expert'), may hold values from 0 to 63, all different within a row; in each aligned block of 40 rows (0 to 39, 40 to 79, ...) at most 7 rows name the same one
- gate_probs: bfloat16 [1280, 8], P('expert'), may hold values from 0.019897461 to 0.5
- w_gate: bfloat16 [32, 3072, 4096], P('expert', 'dp'), may hold values from -0.09375 to 0.09375
- w_up: bfloat16 [32, 3072, 4096], P('expert', 'dp'), may hold values from -0.09375 to 0.09375
- w_down: bfloat16 [32, 3072, 4096], P('expert', 'dp'), may hold values from -0.15625 to 0.15625
Outputs:
- d_tokens: bfloat16 [1280, 4096], P('expert', 'dp')
- d_probs: float32 [1280, 8], P('expert')
The draws below stay inside these ranges and needn't reach their ends.
Inputs may be any that keep to these rules, and one draw needn't show every extreme that they name: `expert_ids`: each row names 8 different experts. The 40 rows of one device (aligned blocks of rows) name no expert more than 7 times, a bound that some block reaches.
All inputs are finite; a program needn't handle non-finite values.
Results may differ from the reference program's by a relative error of at most 0.0061.
Values may be sent and summed in bfloat16 or wider, within the bound.
No kernel may reach another device: no remote copies, remote signals or barrier semaphores. Data moves between devices by JAX's collectives and lax.ppermute only.
A program may use at most 32 MiB of HBM per device.

```python
import math
import jax
import jax.numpy as jnp
import numpy as np
from jax import lax

D = 4096
FF = 1536
TOP = 8
TOK_DEV = 40
EXP_DEV = 2
EXPERTS = 64
SHARDS = 16
FF_DEV = 96
SEND = 7
TOKENS = 1280
N_EXPERT = 32


def block_scale(own_key, shape, pieces, least, largest):
    level, own = 1.0, jax.random.fold_in(own_key, 6)
    for dim, blocks in pieces:
        heights = jnp.exp(jax.random.uniform(jax.random.fold_in(own, dim), (blocks,), jnp.float32, least / len(pieces), largest / len(pieces)))
        level = level * jnp.repeat(heights, shape[dim] // blocks).reshape([-1 if axis == dim else 1 for axis in range(len(shape))])
    return level


def shared_out(rng, own, number, rows, amount, top, most, slope):
    order = jax.random.permutation(rng, amount)
    packed, ordinary = portions_of(amount, rows * top, most, slope, True), portions_of(amount, rows * top, most, slope, False)
    places = jnp.arange(amount)

    def named(lengths, turn):
        used = int((lengths > 0).sum())
        fixed = max(1, used // 4)
        passed = fixed + (places - fixed + turn * (used - fixed)) % max(1, amount - fixed)
        return jnp.zeros((amount,), jnp.int32).at[order[jnp.where(places < fixed, places, passed)]].set(jnp.asarray(lengths, jnp.int32))

    lengths = jnp.where(number % 4 == 0, named(packed, number // 4), named(ordinary, number - number // 4 - 1))
    mixed = jax.random.permutation(jax.random.fold_in(own, 3), amount)
    donor, taker = mixed[0:amount // 2 * 2:2], mixed[1:amount // 2 * 2:2]
    slack = jnp.minimum(lengths[donor] - 1, most - lengths[taker]) // 2
    slack = jnp.where((donor == order[0]) | (taker == order[0]) | (lengths[taker] == 0), 0, jnp.maximum(slack, 0))
    passed = jax.random.randint(jax.random.fold_in(own, 4), (amount // 2,), 0, 1 << 20) % (slack + 1)
    lengths = lengths.at[donor].add(-passed).at[taker].add(passed)
    labels = jnp.searchsorted(jnp.cumsum(lengths), jnp.arange(rows * top), side="right").astype(jnp.int32)
    grid = labels.reshape(top, rows).T
    grid = grid[jax.random.permutation(jax.random.fold_in(own, 1), rows)]
    turn = jax.random.randint(jax.random.fold_in(own, 2), (rows, 1), 0, top)
    return jnp.take_along_axis(grid, (jnp.arange(top)[None, :] + turn) % top, axis=1)


def portions_of(count, total, limit, lean, full):
    portions = [(1 << 20) // math.isqrt(standing ** lean) + 1 for standing in range(1, count + 1)]
    largest = limit if full else min(limit, max(-(-total // count), total * portions[0] // sum(portions)))
    least = 1 if total - largest >= count - 1 else 0
    holding, rest = [largest] + [least] * (count - 1), total - largest - least * (count - 1)
    while rest > 0:
        candidates = [i for i in range(1, count) if holding[i] < largest] or [i for i in range(1, count) if holding[i] < limit]
        pool, remaining = sum([portions[i] for i in candidates]), rest
        for i in candidates:
            more = min(limit - holding[i], max(1, remaining * portions[i] // pool), rest)
            holding[i] = holding[i] + more
            rest = rest - more
    return np.array(holding)


def normal_values(rng, extent, spread, limit, cuts=(), kind=jnp.bfloat16):
    factor_of = block_scale(rng, extent, cuts, -0.22, 0.18) if cuts else 1.0
    values = jax.random.normal(rng, extent, jnp.float32) * spread * factor_of
    return jnp.minimum(jnp.maximum(values, -limit), limit).astype(kind)


def setup_inputs(seed: int = 0) -> dict:
    streams_of = jax.random.split(jax.random.key(seed), 8)
    tokens = normal_values(streams_of[0], (TOKENS, D), 1.0, 6.0, ((0, 32),))
    cotangent = normal_values(streams_of[1], (TOKENS, D), 1.0, 6.0, ((0, 32),))
    expert_ids_keys = jax.random.split(jax.random.fold_in(streams_of[2], 1), TOKENS // TOK_DEV)
    expert_ids_turns = jax.random.permutation(jax.random.fold_in(streams_of[2], 3), TOKENS // TOK_DEV)
    expert_ids = jax.vmap(lambda own, number: shared_out(jax.random.fold_in(streams_of[2], 2), own, number, TOK_DEV, EXPERTS, TOP, SEND, 2))(expert_ids_keys, expert_ids_turns).reshape((TOKENS, TOP))
    gate_probs = jnp.clip(jnp.exp(math.log(0.5) - 3.224016 * jax.random.uniform(streams_of[3], (TOKENS, TOP), jnp.float32) ** block_scale(streams_of[3], (TOKENS, TOP), ((0, 32),), -0.2, 0.2)), 0.019897461, 0.5).astype(jnp.bfloat16)
    w_gate = normal_values(streams_of[4], (N_EXPERT, EXP_DEV * FF, D), D ** -0.5, 0.09375, ((0, 32), (1, 32)))
    w_up = normal_values(streams_of[5], (N_EXPERT, EXP_DEV * FF, D), D ** -0.5, 0.09375, ((0, 32), (1, 32)))
    w_down = normal_values(streams_of[6], (N_EXPERT, EXP_DEV * FF, D), FF ** -0.5, 0.15625, ((0, 32), (1, 32)))
    return {"tokens": tokens, "cotangent": cotangent, "expert_ids": expert_ids, "gate_probs": gate_probs, "w_gate": w_gate, "w_up": w_up, "w_down": w_down}


def reference(tokens, cotangent, expert_ids, gate_probs, w_gate, w_up, w_down):
    flat_ids = expert_ids.reshape(-1)
    flat_probs = gate_probs.reshape(-1)
    capacity = N_EXPERT * SEND
    slot_iota = jnp.arange(capacity, dtype=jnp.int32)
    contract_model = (((1,), (1,)), ((), ()))

    def one_expert(totals, expert):
        token_grads, prob_grads = totals
        matches = flat_ids == expert
        filled = jnp.sum(matches.astype(jnp.int32))
        slot_ids = jnp.nonzero(matches, size=capacity, fill_value=0)[0].astype(jnp.int32)
        usable = slot_iota < filled
        token_of = (slot_ids // TOP).astype(jnp.int32)
        rows_tok = jnp.where(usable[:, None], tokens[token_of], jnp.zeros((), jnp.bfloat16))
        rows_cot = jnp.where(usable[:, None], cotangent[token_of], jnp.zeros((), jnp.bfloat16))
        row_weight = jnp.where(usable, flat_probs[slot_ids].astype(jnp.float32), jnp.float32(0.0))
        group_id = (expert // EXP_DEV).astype(jnp.int32)
        column_start = ((expert % EXP_DEV) * FF).astype(jnp.int32)
        gate_rows = lax.dynamic_slice_in_dim(w_gate[group_id], column_start, FF, 0)
        up_rows = lax.dynamic_slice_in_dim(w_up[group_id], column_start, FF, 0)
        down_rows = lax.dynamic_slice_in_dim(w_down[group_id], column_start, FF, 0)
        pre_gate = lax.dot_general(rows_tok, gate_rows, contract_model, preferred_element_type=jnp.float32)
        pre_up = lax.dot_general(rows_tok, up_rows, contract_model, preferred_element_type=jnp.float32)
        sigmoid_gate = jax.nn.sigmoid(pre_gate)
        activated = pre_gate * sigmoid_gate
        hidden = (activated * pre_up).astype(jnp.bfloat16)
        hid_parts = hidden.astype(jnp.float32).reshape(capacity, SHARDS, FF_DEV)
        down_parts = down_rows.astype(jnp.float32).reshape(SHARDS, FF_DEV, D)
        out_parts = jnp.einsum("rsf,sfd->rsd", hid_parts, down_parts).astype(jnp.bfloat16)
        out_parts = lax.optimization_barrier(out_parts)
        inner_prod = jnp.sum(rows_cot.astype(jnp.float32)[:, None, :] * out_parts.astype(jnp.float32), axis=2).astype(jnp.bfloat16)
        inner_prod = lax.optimization_barrier(inner_prod)
        slot_grad = jnp.sum(inner_prod.astype(jnp.float32), axis=1)
        d_hidden = lax.dot_general(rows_cot, down_rows, contract_model, preferred_element_type=jnp.float32) * row_weight[:, None]
        d_up = (d_hidden * activated).astype(jnp.bfloat16)
        d_gate = (d_hidden * pre_up * sigmoid_gate * (1.0 + pre_gate * (1.0 - sigmoid_gate))).astype(jnp.bfloat16)
        gate_parts = gate_rows.astype(jnp.float32).reshape(SHARDS, FF_DEV, D)
        up_parts = up_rows.astype(jnp.float32).reshape(SHARDS, FF_DEV, D)
        dgate_parts = d_gate.astype(jnp.float32).reshape(capacity, SHARDS, FF_DEV)
        dup_parts = d_up.astype(jnp.float32).reshape(capacity, SHARDS, FF_DEV)
        d_parts = jnp.einsum("rsf,sfd->rsd", dgate_parts, gate_parts) + jnp.einsum("rsf,sfd->rsd", dup_parts, up_parts)
        d_parts = lax.optimization_barrier(d_parts.astype(jnp.bfloat16))
        row_grad = jnp.sum(d_parts.astype(jnp.float32), axis=1)
        row_grad = jnp.where(usable[:, None], row_grad, jnp.float32(0.0))
        token_grads = token_grads.at[token_of].add(row_grad)
        prob_grads = prob_grads.at[slot_ids].add(jnp.where(usable, slot_grad, jnp.float32(0.0)))
        return (token_grads, prob_grads), None

    start = (jnp.zeros((TOKENS, D), jnp.float32), jnp.zeros((TOKENS * TOP,), jnp.float32))
    (token_grads, prob_grads), unused = lax.scan(one_expert, start, jnp.arange(EXPERTS, dtype=jnp.int32))
    return token_grads.astype(jnp.bfloat16), prob_grads.reshape(TOKENS, TOP)
```

```python
import jax
import jax.numpy as jnp
from jax import lax
from jax.sharding import Mesh
from jax.sharding import PartitionSpec as P

FF = 1536
TOP = 8
GROUP = 2
HIGH = lax.Precision.HIGHEST


def slot_tables(expert_ids, shard_type, group_size, dest_count, send_rows):
    tok_rows, top_count = expert_ids.shape
    flat_ids = expert_ids.reshape(-1)
    chosen = flat_ids % group_size == shard_type
    target = flat_ids // group_size
    columns = lax.broadcasted_iota(jnp.int32, (flat_ids.shape[0], dest_count), 1)
    matched = jnp.logical_and(chosen[:, None], target[:, None] == columns).astype(jnp.int32)
    ranking = jnp.sum((jnp.cumsum(matched, axis=0) - 1) * matched, axis=1)
    row_index = jnp.where(chosen, target * send_rows + ranking, -1)
    rows_iota = lax.broadcasted_iota(jnp.int32, (dest_count * send_rows, flat_ids.shape[0]), 0)
    placing = (rows_iota == row_index[None, :]).astype(jnp.bfloat16)
    by_token = placing.reshape(dest_count * send_rows, tok_rows, top_count).sum(axis=2)
    return (placing, by_token)


def shards(tokens, cotangent, expert_ids, gate_probs, w_gate, w_up, w_down):
    dest_count = lax.axis_size("expert")
    shard_width = w_gate.shape[1]
    shard_count = FF // shard_width
    group_size = lax.axis_size("l")
    shard_type = lax.axis_index("l")
    part = lax.axis_index("s")
    tok_rows = tokens.shape[0]
    model_width = tokens.shape[1]
    chunk = model_width // shard_count
    out_width = chunk // group_size
    experts_all = group_size * dest_count
    send_rows = (4 * tok_rows * TOP + 3 * experts_all - 1) // (3 * experts_all)
    slots = dest_count * send_rows
    placing, by_token = slot_tables(expert_ids, shard_type, group_size, dest_count, send_rows)

    tok_chunk = lax.dynamic_slice_in_dim(tokens, part * chunk, chunk, axis=1)
    cot_chunk = lax.dynamic_slice_in_dim(cotangent, part * chunk, chunk, axis=1)
    both_chunk = jnp.concatenate([tok_chunk, cot_chunk], axis=1)
    rows_sent = jnp.dot(by_token, both_chunk, preferred_element_type=jnp.float32).astype(jnp.bfloat16)
    rows_sent = rows_sent.reshape(dest_count, send_rows, 2 * chunk)
    probs_sent = jnp.dot(
        placing, gate_probs.reshape(-1), preferred_element_type=jnp.float32
    ).astype(jnp.bfloat16)
    probs_row = jnp.pad(probs_sent.reshape(dest_count, 1, send_rows), ((0, 0), (0, 0), (0, 2 * chunk - send_rows)))
    payload = jnp.concatenate([rows_sent, probs_row], axis=1)
    recv = lax.all_to_all(payload, "expert", split_axis=0, concat_axis=0, tiled=True)
    probs_in = recv[:, send_rows, :send_rows].reshape(slots).astype(jnp.float32)
    rows_in = recv[:, :send_rows, :].reshape(slots, 2 * chunk)

    gathered = lax.all_gather(rows_in, "s", axis=0, tiled=False)
    tok_parts = gathered[:, :, :chunk]
    cot_parts = gathered[:, :, chunk:]
    rows_tok = tok_parts.transpose(1, 0, 2).reshape(slots, model_width)
    rows_cot = cot_parts.transpose(1, 0, 2).reshape(slots, model_width)
    gate_shard = w_gate[0]
    up_shard = w_up[0]
    down_shard = w_down[0]
    contract_model = (((1,), (1,)), ((), ()))
    pre_gate = lax.dot_general(rows_tok, gate_shard, contract_model, preferred_element_type=jnp.float32)
    pre_up = lax.dot_general(rows_tok, up_shard, contract_model, preferred_element_type=jnp.float32)
    sigmoid_gate = jax.nn.sigmoid(pre_gate)
    activated = pre_gate * sigmoid_gate
    hidden = (activated * pre_up).astype(jnp.bfloat16)
    outputs = jnp.dot(hidden, down_shard, preferred_element_type=jnp.float32).astype(jnp.bfloat16)
    outputs = lax.optimization_barrier(outputs)
    inner = jnp.sum(
        rows_cot.astype(jnp.float32) * outputs.astype(jnp.float32), axis=1
    ).astype(jnp.bfloat16)
    d_hidden = lax.dot_general(rows_cot, down_shard, contract_model, preferred_element_type=jnp.float32)
    d_hidden = d_hidden * probs_in.reshape(-1, 1)
    d_up = (d_hidden * activated).astype(jnp.bfloat16)
    d_gate = (d_hidden * pre_up * sigmoid_gate * (1.0 + pre_gate * (1.0 - sigmoid_gate))).astype(
        jnp.bfloat16
    )
    d_rows = jnp.dot(d_gate, gate_shard, preferred_element_type=jnp.float32) + jnp.dot(
        d_up, up_shard, preferred_element_type=jnp.float32
    )
    d_rows = d_rows.astype(jnp.bfloat16)
    d_split = d_rows.reshape(slots, group_size, shard_count, out_width).transpose(2, 0, 1, 3)
    d_split = d_split.reshape(shard_count, slots, chunk)
    pad_rows = (-(slots + 1)) % 16 + 1
    inner_row = jnp.pad(inner, (0, chunk - slots)).reshape(1, 1, chunk)
    inner_row = jnp.broadcast_to(inner_row, (shard_count, 1, chunk))
    extra = jnp.concatenate(
        [inner_row, jnp.zeros((shard_count, pad_rows - 1, chunk), jnp.bfloat16)], axis=1
    )
    ex_send = jnp.concatenate([d_split, extra], axis=1)
    ex_recv = lax.all_to_all(ex_send, "s", split_axis=0, concat_axis=0, tiled=True)
    summed = jnp.sum(ex_recv.astype(jnp.float32), axis=0)
    grads_chunk = summed[:slots].reshape(dest_count, send_rows, chunk)
    inner_sum = summed[slots, :slots].reshape(dest_count, 1, send_rows)
    inner_sum = jnp.pad(inner_sum, ((0, 0), (0, 0), (0, chunk - send_rows)))
    back_send = jnp.concatenate([grads_chunk, inner_sum], axis=1)
    back = lax.all_to_all(back_send, "expert", split_axis=0, concat_axis=0, tiled=True)

    grads_back = back[:, :send_rows, :].reshape(slots, chunk)
    inner_back = back[:, send_rows, :send_rows].reshape(slots)
    contract_rows = (((0,), (0,)), ((), ()))
    token_terms = lax.dot_general(
        by_token.astype(jnp.float32), grads_back, contract_rows,
        preferred_element_type=jnp.float32, precision=HIGH,
    ).reshape(tok_rows, group_size, out_width)
    slot_terms = lax.dot_general(
        placing.astype(jnp.float32), inner_back, contract_rows,
        preferred_element_type=jnp.float32, precision=HIGH,
    ).reshape(tok_rows, TOP)
    mine = lax.dynamic_index_in_dim(token_terms, shard_type, axis=1, keepdims=False)
    other = lax.dynamic_index_in_dim(token_terms, 1 - shard_type, axis=1, keepdims=False)
    pair_send = jnp.concatenate([other, slot_terms], axis=1)
    pair_recv = lax.ppermute(pair_send, "l", perm=[(0, 1), (1, 0)])
    d_tokens = (mine + pair_recv[:, :out_width]).astype(jnp.bfloat16)
    d_probs = slot_terms + pair_recv[:, out_width:]
    return (d_tokens, d_probs)


def solution(mesh):
    names = mesh.axis_names
    devices = mesh.devices
    if names != ("dp", "expert"):
        devices = devices.transpose([names.index("dp"), names.index("expert")])
    dp_size = devices.shape[0]
    split = Mesh(devices.reshape(GROUP, dp_size // GROUP, devices.shape[1]), ("l", "s", "expert"))
    return jax.shard_map(
        shards,
        mesh=split,
        in_specs=(
            P("expert", None),
            P("expert", None),
            P("expert", None),
            P("expert", None),
            P("expert", ("l", "s"), None),
            P("expert", ("l", "s"), None),
            P("expert", ("l", "s"), None),
        ),
        out_specs=(P("expert", ("l", "s")), P("expert", None)),
        check_vma=False,
    )
```

```python
import jax
import jax.numpy as jnp
from jax import lax
from jax.sharding import Mesh
from jax.sharding import PartitionSpec as P

FF = 1536
TOP = 8
GROUP = 2
HIGH = lax.Precision.HIGHEST


def slot_tables(expert_ids, shard_type, group_size, dest_count, send_rows):
    tok_rows, top_count = expert_ids.shape
    flat_ids = expert_ids.reshape(-1)
    chosen = flat_ids % group_size == shard_type
    target = flat_ids // group_size
    columns = lax.broadcasted_iota(jnp.int32, (flat_ids.shape[0], dest_count), 1)
    matched = jnp.logical_and(chosen[:, None], target[:, None] == columns).astype(jnp.int32)
    ranking = jnp.sum((jnp.cumsum(matched, axis=0) - 1) * matched, axis=1)
    row_index = jnp.where(chosen, target * send_rows + ranking, -1)
    rows_iota = lax.broadcasted_iota(jnp.int32, (dest_count * send_rows, flat_ids.shape[0]), 0)
    placing = (rows_iota == row_index[None, :]).astype(jnp.bfloat16)
    by_token = placing.reshape(dest_count * send_rows, tok_rows, top_count).sum(axis=2)
    return (placing, by_token)


def shards(tokens, cotangent, expert_ids, gate_probs, w_gate, w_up, w_down):
    dest_count = lax.axis_size("expert")
    shard_width = w_gate.shape[1]
    shard_count = FF // shard_width
    group_size = lax.axis_size("l")
    shard_type = lax.axis_index("l")
    part = lax.axis_index("s")
    tok_rows = tokens.shape[0]
    model_width = tokens.shape[1]
    chunk = model_width // shard_count
    out_width = chunk // group_size
    experts_all = group_size * dest_count
    send_rows = (4 * tok_rows * TOP + 3 * experts_all - 1) // (3 * experts_all)
    slots = dest_count * send_rows
    placing, by_token = slot_tables(expert_ids, shard_type, group_size, dest_count, send_rows)

    tok_chunk = lax.dynamic_slice_in_dim(tokens, part * chunk, chunk, axis=1)
    cot_chunk = lax.dynamic_slice_in_dim(cotangent, part * chunk, chunk, axis=1)
    both_chunk = jnp.concatenate([tok_chunk, cot_chunk], axis=1)
    rows_sent = jnp.dot(by_token, both_chunk, preferred_element_type=jnp.float32).astype(jnp.bfloat16)
    rows_sent = rows_sent.reshape(dest_count, send_rows, 2 * chunk)
    probs_sent = jnp.dot(
        placing, gate_probs.reshape(-1), preferred_element_type=jnp.float32
    ).astype(jnp.bfloat16)
    probs_row = jnp.pad(probs_sent.reshape(dest_count, 1, send_rows), ((0, 0), (0, 0), (0, 2 * chunk - send_rows)))
    payload = jnp.concatenate([rows_sent, probs_row], axis=1)
    recv = lax.all_to_all(payload, "expert", split_axis=0, concat_axis=0, tiled=True)
    probs_in = recv[:, send_rows, :send_rows].reshape(slots).astype(jnp.float32)
    rows_in = recv[:, :send_rows, :].reshape(slots, 2 * chunk)

    gathered = lax.all_gather(rows_in, "s", axis=0, tiled=False)
    tok_parts = gathered[:, :, :chunk]
    cot_parts = gathered[:, :, chunk:]
    rows_tok = tok_parts.transpose(1, 0, 2).reshape(slots, model_width)
    rows_cot = cot_parts.transpose(1, 0, 2).reshape(slots, model_width)
    gate_shard = w_gate[0]
    up_shard = w_up[0]
    down_shard = w_down[0]
    contract_model = (((1,), (1,)), ((), ()))
    pre_gate = lax.dot_general(rows_tok, gate_shard, contract_model, preferred_element_type=jnp.float32)
    pre_up = lax.dot_general(rows_tok, up_shard, contract_model, preferred_element_type=jnp.float32)
    sigmoid_gate = jax.nn.sigmoid(pre_gate)
    activated = pre_gate * sigmoid_gate
    hidden = (activated * pre_up).astype(jnp.bfloat16)
    outputs = jnp.dot(hidden, down_shard, preferred_element_type=jnp.float32).astype(jnp.bfloat16)
    outputs = lax.optimization_barrier(outputs)
    inner = jnp.sum(
        rows_cot.astype(jnp.float32) * outputs.astype(jnp.float32), axis=1
    ).astype(jnp.bfloat16)
    d_hidden = lax.dot_general(rows_cot, down_shard, contract_model, preferred_element_type=jnp.float32)
    d_hidden = d_hidden * probs_in.reshape(-1, 1)
    d_up = (d_hidden * activated).astype(jnp.bfloat16)
    d_gate = (d_hidden * pre_up * sigmoid_gate * (1.0 + pre_gate * (1.0 - sigmoid_gate))).astype(
        jnp.bfloat16
    )
    d_rows = jnp.dot(d_gate, gate_shard, preferred_element_type=jnp.float32) + jnp.dot(
        d_up, up_shard, preferred_element_type=jnp.float32
    )
    d_rows = d_rows.astype(jnp.bfloat16)
    d_split = d_rows.reshape(slots, group_size, shard_count, out_width).transpose(2, 0, 1, 3)
    d_split = d_split.reshape(shard_count, slots, chunk)
    pad_rows = (-(slots + 1)) % 16 + 1
    inner_row = jnp.pad(inner, (0, chunk - slots)).reshape(1, 1, chunk)
    inner_row = jnp.broadcast_to(inner_row, (shard_count, 1, chunk))
    extra = jnp.concatenate(
        [inner_row, jnp.zeros((shard_count, pad_rows - 1, chunk), jnp.bfloat16)], axis=1
    )
    ex_send = jnp.concatenate([d_split, extra], axis=1)
    ex_recv = lax.all_to_all(ex_send, "s", split_axis=0, concat_axis=0, tiled=True)
    summed = jnp.sum(ex_recv.astype(jnp.float32), axis=0)
    grads_chunk = summed[:slots].reshape(dest_count, send_rows, chunk)
    inner_sum = summed[slots, :slots].reshape(dest_count, send_rows)
    inner_hi = inner_sum.astype(jnp.bfloat16)
    inner_lo = (inner_sum - inner_hi.astype(jnp.float32)).astype(jnp.bfloat16)
    inner_pair = jnp.concatenate([inner_hi, inner_lo], axis=1).reshape(dest_count, 1, 2 * send_rows)
    inner_pair = jnp.pad(inner_pair, ((0, 0), (0, 0), (0, chunk - 2 * send_rows)))
    back_send = jnp.concatenate([grads_chunk.astype(jnp.bfloat16), inner_pair], axis=1)
    back = lax.all_to_all(back_send, "expert", split_axis=0, concat_axis=0, tiled=True)

    grads_back = back[:, :send_rows, :].reshape(slots, chunk)
    inner_back = back[:, send_rows, :2 * send_rows].astype(jnp.float32)
    inner_back = (inner_back[:, :send_rows] + inner_back[:, send_rows:]).reshape(slots)
    contract_rows = (((0,), (0,)), ((), ()))
    token_terms = lax.dot_general(
        by_token, grads_back, contract_rows, preferred_element_type=jnp.float32
    ).reshape(tok_rows, group_size, out_width)
    slot_terms = lax.dot_general(
        placing.astype(jnp.float32), inner_back, contract_rows,
        preferred_element_type=jnp.float32, precision=HIGH,
    ).reshape(tok_rows, TOP)
    mine = lax.dynamic_index_in_dim(token_terms, shard_type, axis=1, keepdims=False)
    other = lax.dynamic_index_in_dim(token_terms, 1 - shard_type, axis=1, keepdims=False)
    pair_send = jnp.concatenate([other, slot_terms], axis=1)
    pair_recv = lax.ppermute(pair_send, "l", perm=[(0, 1), (1, 0)])
    d_tokens = (mine + pair_recv[:, :out_width]).astype(jnp.bfloat16)
    d_probs = slot_terms + pair_recv[:, out_width:]
    return (d_tokens, d_probs)


def solution(mesh):
    names = mesh.axis_names
    devices = mesh.devices
    if names != ("dp", "expert"):
        devices = devices.transpose([names.index("dp"), names.index("expert")])
    dp_size = devices.shape[0]
    split = Mesh(devices.reshape(GROUP, dp_size // GROUP, devices.shape[1]), ("l", "s", "expert"))
    return jax.shard_map(
        shards,
        mesh=split,
        in_specs=(
            P("expert", None),
            P("expert", None),
            P("expert", None),
            P("expert", None),
            P("expert", ("l", "s"), None),
            P("expert", ("l", "s"), None),
            P("expert", ("l", "s"), None),
        ),
        out_specs=(P("expert", ("l", "s")), P("expert", None)),
        check_vma=False,
    )
```

```python
import jax
import jax.numpy as jnp
from jax import lax
from jax.sharding import Mesh
from jax.sharding import PartitionSpec as P

FF = 1536
TOP = 8
GROUP = 2
HIGH = lax.Precision.HIGHEST


def slot_tables(expert_ids, shard_type, group_size, dest_count, send_rows):
    tok_rows, top_count = expert_ids.shape
    flat_ids = expert_ids.reshape(-1)
    chosen = flat_ids % group_size == shard_type
    target = flat_ids // group_size
    columns = lax.broadcasted_iota(jnp.int32, (flat_ids.shape[0], dest_count), 1)
    matched = jnp.logical_and(chosen[:, None], target[:, None] == columns).astype(jnp.int32)
    ranking = jnp.sum((jnp.cumsum(matched, axis=0) - 1) * matched, axis=1)
    row_index = jnp.where(chosen, target * send_rows + ranking, -1)
    rows_iota = lax.broadcasted_iota(jnp.int32, (dest_count * send_rows, flat_ids.shape[0]), 0)
    placing = (rows_iota == row_index[None, :]).astype(jnp.bfloat16)
    by_token = placing.reshape(dest_count * send_rows, tok_rows, top_count).sum(axis=2)
    return (placing, by_token)


def z_exchange(x):
    nh = lax.axis_size("zh")
    nl = lax.axis_size("zl")
    ih = lax.axis_index("zh")
    rest = x.shape[1:]
    x4 = x.reshape((nh, nl) + rest)
    y = lax.dynamic_slice_in_dim(jnp.concatenate([x4, x4], axis=0), ih, nh, axis=0)
    parts = [y[0]]
    for d in range(1, nh):
        parts.append(lax.ppermute(y[d], "zh", perm=[(h, (h + d) % nh) for h in range(nh)]))
    z = jnp.stack(parts, axis=1)
    w = lax.all_to_all(z, "zl", split_axis=0, concat_axis=0, tiled=True)
    w_rev = w[:, ::-1]
    v = lax.dynamic_slice_in_dim(jnp.concatenate([w_rev, w_rev], axis=1), (nh - 1 - ih) % nh, nh, axis=1)
    return jnp.swapaxes(v, 0, 1).reshape((nh * nl,) + rest)


def shards(tokens, cotangent, expert_ids, gate_probs, w_gate, w_up, w_down):
    dest_count = lax.axis_size("zh") * lax.axis_size("zl")
    shard_width = w_gate.shape[1]
    shard_count = FF // shard_width
    group_size = lax.axis_size("l")
    shard_type = lax.axis_index("l")
    part = lax.axis_index("s")
    tok_rows = tokens.shape[0]
    model_width = tokens.shape[1]
    chunk = model_width // shard_count
    out_width = chunk // group_size
    experts_all = group_size * dest_count
    send_rows = (4 * tok_rows * TOP + 3 * experts_all - 1) // (3 * experts_all)
    slots = dest_count * send_rows
    placing, by_token = slot_tables(expert_ids, shard_type, group_size, dest_count, send_rows)

    tok_chunk = lax.dynamic_slice_in_dim(tokens, part * chunk, chunk, axis=1)
    cot_chunk = lax.dynamic_slice_in_dim(cotangent, part * chunk, chunk, axis=1)
    both_chunk = jnp.concatenate([tok_chunk, cot_chunk], axis=1)
    rows_sent = jnp.dot(by_token, both_chunk, preferred_element_type=jnp.float32).astype(jnp.bfloat16)
    rows_sent = rows_sent.reshape(dest_count, send_rows, 2 * chunk)
    probs_sent = jnp.dot(
        placing, gate_probs.reshape(-1), preferred_element_type=jnp.float32
    ).astype(jnp.bfloat16)
    probs_row = jnp.pad(probs_sent.reshape(dest_count, 1, send_rows), ((0, 0), (0, 0), (0, 2 * chunk - send_rows)))
    payload = jnp.concatenate([rows_sent, probs_row], axis=1)
    recv = z_exchange(payload)
    probs_in = recv[:, send_rows, :send_rows].reshape(slots).astype(jnp.float32)
    rows_in = recv[:, :send_rows, :].reshape(slots, 2 * chunk)

    gathered = lax.all_gather(rows_in, "s", axis=0, tiled=False)
    tok_parts = gathered[:, :, :chunk]
    cot_parts = gathered[:, :, chunk:]
    rows_tok = tok_parts.transpose(1, 0, 2).reshape(slots, model_width)
    rows_cot = cot_parts.transpose(1, 0, 2).reshape(slots, model_width)
    gate_shard = w_gate[0]
    up_shard = w_up[0]
    down_shard = w_down[0]
    contract_model = (((1,), (1,)), ((), ()))
    pre_gate = lax.dot_general(rows_tok, gate_shard, contract_model, preferred_element_type=jnp.float32)
    pre_up = lax.dot_general(rows_tok, up_shard, contract_model, preferred_element_type=jnp.float32)
    sigmoid_gate = jax.nn.sigmoid(pre_gate)
    activated = pre_gate * sigmoid_gate
    hidden = (activated * pre_up).astype(jnp.bfloat16)
    outputs = jnp.dot(hidden, down_shard, preferred_element_type=jnp.float32).astype(jnp.bfloat16)
    outputs = lax.optimization_barrier(outputs)
    inner = jnp.sum(
        rows_cot.astype(jnp.float32) * outputs.astype(jnp.float32), axis=1
    ).astype(jnp.bfloat16)
    d_hidden = lax.dot_general(rows_cot, down_shard, contract_model, preferred_element_type=jnp.float32)
    d_hidden = d_hidden * probs_in.reshape(-1, 1)
    d_up = (d_hidden * activated).astype(jnp.bfloat16)
    d_gate = (d_hidden * pre_up * sigmoid_gate * (1.0 + pre_gate * (1.0 - sigmoid_gate))).astype(
        jnp.bfloat16
    )
    d_rows = jnp.dot(d_gate, gate_shard, preferred_element_type=jnp.float32) + jnp.dot(
        d_up, up_shard, preferred_element_type=jnp.float32
    )
    d_rows = d_rows.astype(jnp.bfloat16)
    d_split = d_rows.reshape(slots, group_size, shard_count, out_width).transpose(2, 0, 1, 3)
    d_split = d_split.reshape(shard_count, slots, chunk)
    pad_rows = (-(slots + 1)) % 16 + 1
    inner_row = jnp.pad(inner, (0, chunk - slots)).reshape(1, 1, chunk)
    inner_row = jnp.broadcast_to(inner_row, (shard_count, 1, chunk))
    extra = jnp.concatenate(
        [inner_row, jnp.zeros((shard_count, pad_rows - 1, chunk), jnp.bfloat16)], axis=1
    )
    ex_send = jnp.concatenate([d_split, extra], axis=1)
    ex_recv = lax.all_to_all(ex_send, "s", split_axis=0, concat_axis=0, tiled=True)
    summed = jnp.sum(ex_recv.astype(jnp.float32), axis=0)
    grads_chunk = summed[:slots].reshape(dest_count, send_rows, chunk)
    inner_sum = summed[slots, :slots].reshape(dest_count, send_rows)
    inner_hi = inner_sum.astype(jnp.bfloat16)
    inner_lo = (inner_sum - inner_hi.astype(jnp.float32)).astype(jnp.bfloat16)
    inner_pair = jnp.concatenate([inner_hi, inner_lo], axis=1).reshape(dest_count, 1, 2 * send_rows)
    inner_pair = jnp.pad(inner_pair, ((0, 0), (0, 0), (0, chunk - 2 * send_rows)))
    back_send = jnp.concatenate([grads_chunk.astype(jnp.bfloat16), inner_pair], axis=1)
    back = z_exchange(back_send)

    grads_back = back[:, :send_rows, :].reshape(slots, chunk)
    inner_back = back[:, send_rows, :2 * send_rows].astype(jnp.float32)
    inner_back = (inner_back[:, :send_rows] + inner_back[:, send_rows:]).reshape(slots)
    contract_rows = (((0,), (0,)), ((), ()))
    token_terms = lax.dot_general(
        by_token, grads_back, contract_rows, preferred_element_type=jnp.float32
    ).reshape(tok_rows, group_size, out_width)
    slot_terms = lax.dot_general(
        placing.astype(jnp.float32), inner_back, contract_rows,
        preferred_element_type=jnp.float32, precision=HIGH,
    ).reshape(tok_rows, TOP)
    mine = lax.dynamic_index_in_dim(token_terms, shard_type, axis=1, keepdims=False)
    other = lax.dynamic_index_in_dim(token_terms, 1 - shard_type, axis=1, keepdims=False)
    pair_send = jnp.concatenate([other, slot_terms], axis=1)
    pair_recv = lax.ppermute(pair_send, "l", perm=[(0, 1), (1, 0)])
    d_tokens = (mine + pair_recv[:, :out_width]).astype(jnp.bfloat16)
    d_probs = slot_terms + pair_recv[:, out_width:]
    return (d_tokens, d_probs)


def solution(mesh):
    names = mesh.axis_names
    devices = mesh.devices
    if names != ("dp", "expert"):
        devices = devices.transpose([names.index("dp"), names.index("expert")])
    dp_size = devices.shape[0]
    z_size = devices.shape[1]
    z_low = 8 if z_size % 8 == 0 else z_size
    split = Mesh(
        devices.reshape(GROUP, dp_size // GROUP, z_size // z_low, z_low), ("l", "s", "zh", "zl")
    )
    return jax.shard_map(
        shards,
        mesh=split,
        in_specs=(
            P(("zh", "zl"), None),
            P(("zh", "zl"), None),
            P(("zh", "zl"), None),
            P(("zh", "zl"), None),
            P(("zh", "zl"), ("l", "s"), None),
            P(("zh", "zl"), ("l", "s"), None),
            P(("zh", "zl"), ("l", "s"), None),
        ),
        out_specs=(P(("zh", "zl"), ("l", "s")), P(("zh", "zl"), None)),
        check_vma=False,
    )
```

```python
import jax
import jax.numpy as jnp
from jax import lax
from jax.sharding import Mesh
from jax.sharding import PartitionSpec as P

FF = 1536
TOP = 8
GROUP = 2
HIGH = lax.Precision.HIGHEST


def slot_tables(expert_ids, shard_type, group_size, dest_count, send_rows):
    tok_rows, top_count = expert_ids.shape
    flat_ids = expert_ids.reshape(-1)
    chosen = flat_ids % group_size == shard_type
    target = flat_ids // group_size
    columns = lax.broadcasted_iota(jnp.int32, (flat_ids.shape[0], dest_count), 1)
    matched = jnp.logical_and(chosen[:, None], target[:, None] == columns).astype(jnp.int32)
    ranking = jnp.sum((jnp.cumsum(matched, axis=0) - 1) * matched, axis=1)
    row_index = jnp.where(chosen, target * send_rows + ranking, -1)
    rows_iota = lax.broadcasted_iota(jnp.int32, (dest_count * send_rows, flat_ids.shape[0]), 0)
    placing = (rows_iota == row_index[None, :]).astype(jnp.bfloat16)
    by_token = placing.reshape(dest_count * send_rows, tok_rows, top_count).sum(axis=2)
    return (placing, by_token)


def shards(tokens, cotangent, expert_ids, gate_probs, w_gate, w_up, w_down):
    dest_count = lax.axis_size("expert")
    shard_width = w_gate.shape[1]
    shard_count = FF // shard_width
    group_size = lax.axis_size("l")
    shard_type = lax.axis_index("l")
    part = lax.axis_index("s")
    tok_rows = tokens.shape[0]
    model_width = tokens.shape[1]
    chunk = model_width // shard_count
    out_width = chunk // group_size
    experts_all = group_size * dest_count
    send_rows = (4 * tok_rows * TOP + 3 * experts_all - 1) // (3 * experts_all)
    slots = dest_count * send_rows
    placing, by_token = slot_tables(expert_ids, shard_type, group_size, dest_count, send_rows)

    tok_chunk = lax.dynamic_slice_in_dim(tokens, part * chunk, chunk, axis=1)
    cot_chunk = lax.dynamic_slice_in_dim(cotangent, part * chunk, chunk, axis=1)
    both_chunk = jnp.concatenate([tok_chunk, cot_chunk], axis=1)
    rows_sent = jnp.dot(by_token, both_chunk, preferred_element_type=jnp.float32).astype(jnp.bfloat16)
    rows_sent = rows_sent.reshape(dest_count, send_rows, 2 * chunk)
    probs_sent = jnp.dot(
        placing, gate_probs.reshape(-1), preferred_element_type=jnp.float32
    ).astype(jnp.bfloat16)
    probs_row = jnp.pad(probs_sent.reshape(dest_count, 1, send_rows), ((0, 0), (0, 0), (0, 2 * chunk - send_rows)))
    payload = jnp.concatenate([rows_sent, probs_row], axis=1)
    recv = lax.all_to_all(payload, "expert", split_axis=0, concat_axis=0, tiled=True)
    probs_in = recv[:, send_rows, :send_rows].reshape(slots).astype(jnp.float32)
    rows_in = recv[:, :send_rows, :].reshape(slots, 2 * chunk)

    gathered = lax.all_gather(rows_in, "s", axis=0, tiled=False)
    tok_parts = gathered[:, :, :chunk]
    cot_parts = gathered[:, :, chunk:]
    rows_tok = tok_parts.transpose(1, 0, 2).reshape(slots, model_width)
    rows_cot = cot_parts.transpose(1, 0, 2).reshape(slots, model_width)
    gate_shard = w_gate[0]
    up_shard = w_up[0]
    down_shard = w_down[0]
    contract_model = (((1,), (1,)), ((), ()))
    pre_gate = lax.dot_general(rows_tok, gate_shard, contract_model, preferred_element_type=jnp.float32)
    pre_up = lax.dot_general(rows_tok, up_shard, contract_model, preferred_element_type=jnp.float32)
    sigmoid_gate = jax.nn.sigmoid(pre_gate)
    activated = pre_gate * sigmoid_gate
    hidden = (activated * pre_up).astype(jnp.bfloat16)
    outputs = jnp.dot(hidden, down_shard, preferred_element_type=jnp.float32).astype(jnp.bfloat16)
    outputs = lax.optimization_barrier(outputs)
    inner = jnp.sum(
        rows_cot.astype(jnp.float32) * outputs.astype(jnp.float32), axis=1
    ).astype(jnp.bfloat16)
    d_hidden = lax.dot_general(rows_cot, down_shard, contract_model, preferred_element_type=jnp.float32)
    d_hidden = d_hidden * probs_in.reshape(-1, 1)
    d_up = (d_hidden * activated).astype(jnp.bfloat16)
    d_gate = (d_hidden * pre_up * sigmoid_gate * (1.0 + pre_gate * (1.0 - sigmoid_gate))).astype(
        jnp.bfloat16
    )
    d_rows = jnp.dot(d_gate, gate_shard, preferred_element_type=jnp.float32) + jnp.dot(
        d_up, up_shard, preferred_element_type=jnp.float32
    )
    d_rows = d_rows.astype(jnp.bfloat16)
    dp_count = group_size * shard_count
    d_split = d_rows.reshape(slots, dp_count, out_width).transpose(1, 0, 2)
    inner_rows = -(-slots // out_width)
    pad_rows = (-(slots + inner_rows)) % 16
    inner_block = jnp.pad(inner, (0, inner_rows * out_width - slots)).reshape(1, inner_rows, out_width)
    extra = jnp.concatenate(
        [inner_block, jnp.zeros((1, pad_rows, out_width), jnp.bfloat16)], axis=1
    )
    extra = jnp.broadcast_to(extra, (dp_count,) + extra.shape[1:])
    ex_send = jnp.concatenate([d_split, extra], axis=1)
    ex_recv = lax.all_to_all(ex_send, ("l", "s"), split_axis=0, concat_axis=0, tiled=True)
    ex_recv = ex_recv.reshape((group_size, shard_count) + ex_recv.shape[1:])
    summed = jnp.sum(ex_recv.astype(jnp.float32), axis=1)
    grads_chunk = summed[:, :slots].reshape(group_size, dest_count, send_rows, out_width)
    grads_chunk = grads_chunk.transpose(1, 0, 2, 3).astype(jnp.bfloat16)
    inner_sum = summed[:, slots:slots + inner_rows].reshape(group_size, inner_rows * out_width)
    inner_sum = inner_sum[:, :slots].reshape(group_size, dest_count, send_rows).transpose(1, 0, 2)
    inner_hi = inner_sum.astype(jnp.bfloat16)
    inner_lo = (inner_sum - inner_hi.astype(jnp.float32)).astype(jnp.bfloat16)
    inner_pair = jnp.concatenate([inner_hi, inner_lo], axis=2).reshape(dest_count, group_size, 1, 2 * send_rows)
    inner_pair = jnp.pad(inner_pair, ((0, 0), (0, 0), (0, 0), (0, out_width - 2 * send_rows)))
    back_send = jnp.concatenate([grads_chunk, inner_pair], axis=2)
    back = lax.all_to_all(back_send, "expert", split_axis=0, concat_axis=0, tiled=True)

    back = back.transpose(1, 0, 2, 3)
    grads_back = back[:, :, :send_rows, :].reshape(group_size * slots, out_width)
    inner_back = back[:, :, send_rows, :2 * send_rows].astype(jnp.float32)
    inner_back = (inner_back[:, :, :send_rows] + inner_back[:, :, send_rows:]).reshape(group_size * slots)
    tables = [slot_tables(expert_ids, kind, group_size, dest_count, send_rows) for kind in range(group_size)]
    placing_all = jnp.concatenate([t[0] for t in tables], axis=0)
    by_token_all = jnp.concatenate([t[1] for t in tables], axis=0)
    contract_rows = (((0,), (0,)), ((), ()))
    d_tokens = lax.dot_general(
        by_token_all, grads_back, contract_rows, preferred_element_type=jnp.float32
    ).astype(jnp.bfloat16)
    d_probs = lax.dot_general(
        placing_all.astype(jnp.float32), inner_back, contract_rows,
        preferred_element_type=jnp.float32, precision=HIGH,
    ).reshape(tok_rows, TOP)
    return (d_tokens, d_probs)


def solution(mesh):
    names = mesh.axis_names
    devices = mesh.devices
    if names != ("dp", "expert"):
        devices = devices.transpose([names.index("dp"), names.index("expert")])
    dp_size = devices.shape[0]
    split = Mesh(devices.reshape(GROUP, dp_size // GROUP, devices.shape[1]), ("l", "s", "expert"))
    return jax.shard_map(
        shards,
        mesh=split,
        in_specs=(
            P("expert", None),
            P("expert", None),
            P("expert", None),
            P("expert", None),
            P("expert", ("l", "s"), None),
            P("expert", ("l", "s"), None),
            P("expert", ("l", "s"), None),
        ),
        out_specs=(P("expert", ("l", "s")), P("expert", None)),
        check_vma=False,
    )
```

```python
import jax
import jax.numpy as jnp
from jax import lax
from jax.sharding import Mesh
from jax.sharding import PartitionSpec as P

FF = 1536
TOP = 8
GROUP = 2


def slot_tables(expert_ids, shard_type, group_size, dest_count, send_rows):
    tok_rows, top_count = expert_ids.shape
    flat_ids = expert_ids.reshape(-1)
    chosen = flat_ids % group_size == shard_type
    target = flat_ids // group_size
    columns = lax.broadcasted_iota(jnp.int32, (flat_ids.shape[0], dest_count), 1)
    matched = jnp.logical_and(chosen[:, None], target[:, None] == columns).astype(jnp.int32)
    ranking = jnp.sum((jnp.cumsum(matched, axis=0) - 1) * matched, axis=1)
    row_index = jnp.where(chosen, target * send_rows + ranking, -1)
    rows_iota = lax.broadcasted_iota(jnp.int32, (dest_count * send_rows, flat_ids.shape[0]), 0)
    placing = (rows_iota == row_index[None, :]).astype(jnp.bfloat16)
    by_token = placing.reshape(dest_count * send_rows, tok_rows, top_count).sum(axis=2)
    return (placing, by_token)


def shards(tokens, cotangent, expert_ids, gate_probs, w_gate, w_up, w_down):
    dest_count = lax.axis_size("expert")
    shard_width = w_gate.shape[1]
    shard_count = FF // shard_width
    group_size = lax.axis_size("l")
    shard_type = lax.axis_index("l")
    part = (lax.axis_index("sy") * lax.axis_size("sx") + lax.axis_index("sx")) * lax.axis_size("c") + lax.axis_index("c")
    core = lax.axis_index("c")
    tok_rows = tokens.shape[0]
    model_width = tokens.shape[1]
    chunk = model_width // shard_count
    out_width = chunk // group_size
    experts_all = group_size * dest_count
    send_rows = (4 * tok_rows * TOP + 3 * experts_all - 1) // (3 * experts_all)
    slots = dest_count * send_rows
    tables = [slot_tables(expert_ids, kind, group_size, dest_count, send_rows) for kind in range(group_size)]
    placing_all = jnp.concatenate([t[0] for t in tables], axis=0)
    by_token_all = jnp.concatenate([t[1] for t in tables], axis=0)
    placing = lax.dynamic_slice_in_dim(placing_all, shard_type * slots, slots, axis=0)
    by_token = lax.dynamic_slice_in_dim(by_token_all, shard_type * slots, slots, axis=0)

    tok_chunk = lax.dynamic_slice_in_dim(tokens, part * chunk, chunk, axis=1)
    cot_chunk = lax.dynamic_slice_in_dim(cotangent, part * chunk, chunk, axis=1)
    both_chunk = jnp.concatenate([tok_chunk, cot_chunk], axis=1)
    rows_sent = jnp.dot(by_token, both_chunk, preferred_element_type=jnp.float32).astype(jnp.bfloat16)
    rows_sent = rows_sent.reshape(dest_count, send_rows, 2 * chunk)
    probs_sent = jnp.dot(
        placing, gate_probs.reshape(-1), preferred_element_type=jnp.float32
    ).astype(jnp.bfloat16)
    probs_row = jnp.pad(probs_sent.reshape(dest_count, 1, send_rows), ((0, 0), (0, 0), (0, 2 * chunk - send_rows)))
    payload = jnp.concatenate([rows_sent, probs_row], axis=1)
    recv = lax.all_to_all(payload, "expert", split_axis=0, concat_axis=0, tiled=True)
    probs_in = recv[:, send_rows, :send_rows].reshape(slots).astype(jnp.float32)
    rows_in = recv[:, :send_rows, :].reshape(slots, 2 * chunk)

    chips = lax.axis_size("sy") * lax.axis_size("sx")
    spread = jnp.broadcast_to(rows_in[None], (chips,) + rows_in.shape)
    same_core = lax.all_to_all(spread, ("sy", "sx"), split_axis=0, concat_axis=0, tiled=True)
    other_core = lax.ppermute(same_core, "c", perm=[(0, 1), (1, 0)])
    by_core = jnp.stack([same_core, other_core, same_core], axis=1)
    gathered = lax.dynamic_slice_in_dim(by_core, core, 2, axis=1).reshape((shard_count,) + rows_in.shape)
    tok_parts = gathered[:, :, :chunk]
    cot_parts = gathered[:, :, chunk:]
    rows_tok = tok_parts.transpose(1, 0, 2).reshape(slots, model_width)
    rows_cot = cot_parts.transpose(1, 0, 2).reshape(slots, model_width)
    gate_shard = w_gate[0]
    up_shard = w_up[0]
    down_shard = w_down[0]
    contract_model = (((1,), (1,)), ((), ()))
    pre_gate = lax.dot_general(rows_tok, gate_shard, contract_model, preferred_element_type=jnp.float32)
    pre_up = lax.dot_general(rows_tok, up_shard, contract_model, preferred_element_type=jnp.float32)
    sigmoid_gate = jax.nn.sigmoid(pre_gate)
    activated = pre_gate * sigmoid_gate
    hidden = (activated * pre_up).astype(jnp.bfloat16)
    outputs = jnp.dot(hidden, down_shard, preferred_element_type=jnp.float32).astype(jnp.bfloat16)
    outputs = lax.optimization_barrier(outputs)
    inner = jnp.sum(
        rows_cot.astype(jnp.float32) * outputs.astype(jnp.float32), axis=1
    ).astype(jnp.bfloat16)
    d_hidden = lax.dot_general(rows_cot, down_shard, contract_model, preferred_element_type=jnp.float32)
    d_hidden = d_hidden * probs_in.reshape(-1, 1)
    d_up = (d_hidden * activated).astype(jnp.bfloat16)
    d_gate = (d_hidden * pre_up * sigmoid_gate * (1.0 + pre_gate * (1.0 - sigmoid_gate))).astype(
        jnp.bfloat16
    )
    d_rows = jnp.dot(d_gate, gate_shard, preferred_element_type=jnp.float32) + jnp.dot(
        d_up, up_shard, preferred_element_type=jnp.float32
    )
    d_rows = d_rows.astype(jnp.bfloat16)
    dp_count = group_size * shard_count
    d_split = d_rows.reshape(slots, dp_count, out_width).transpose(1, 0, 2)
    inner_rows = -(-slots // out_width)
    pad_rows = (-(slots + inner_rows)) % 16
    inner_block = jnp.pad(inner, (0, inner_rows * out_width - slots)).reshape(1, inner_rows, out_width)
    extra = jnp.concatenate(
        [inner_block, jnp.zeros((1, pad_rows, out_width), jnp.bfloat16)], axis=1
    )
    extra = jnp.broadcast_to(extra, (dp_count,) + extra.shape[1:])
    ex_send = jnp.concatenate([d_split, extra], axis=1)
    ex_recv = lax.all_to_all(ex_send, ("l", "sy", "sx", "c"), split_axis=0, concat_axis=0, tiled=True)
    ex_recv = ex_recv.reshape((group_size, shard_count) + ex_recv.shape[1:])
    summed = jnp.sum(ex_recv.astype(jnp.float32), axis=1)
    grads_chunk = summed[:, :slots].reshape(group_size, dest_count, send_rows, out_width)
    grads_chunk = grads_chunk.transpose(1, 0, 2, 3).astype(jnp.bfloat16)
    inner_sum = summed[:, slots:slots + inner_rows].reshape(group_size, inner_rows * out_width)
    inner_sum = inner_sum[:, :slots].reshape(group_size, dest_count, send_rows).transpose(1, 0, 2)
    inner_hi = inner_sum.astype(jnp.bfloat16)
    inner_lo = (inner_sum - inner_hi.astype(jnp.float32)).astype(jnp.bfloat16)
    inner_pair = jnp.concatenate([inner_hi, inner_lo], axis=2).reshape(dest_count, group_size, 1, 2 * send_rows)
    inner_pair = jnp.pad(inner_pair, ((0, 0), (0, 0), (0, 0), (0, out_width - 2 * send_rows)))
    back_send = jnp.concatenate([grads_chunk, inner_pair], axis=2)
    back = lax.all_to_all(back_send, "expert", split_axis=0, concat_axis=0, tiled=True)

    back = back.transpose(1, 0, 2, 3)
    grads_back = back[:, :, :send_rows, :].reshape(group_size * slots, out_width)
    inner_back = back[:, :, send_rows, :2 * send_rows]
    inner_hi = inner_back[:, :, :send_rows].reshape(group_size * slots)
    inner_lo = inner_back[:, :, send_rows:].reshape(group_size * slots)
    contract_rows = (((0,), (0,)), ((), ()))
    d_tokens = lax.dot_general(
        by_token_all, grads_back, contract_rows, preferred_element_type=jnp.float32
    ).astype(jnp.bfloat16)
    d_probs = lax.dot_general(
        placing_all, inner_hi, contract_rows, preferred_element_type=jnp.float32
    ) + lax.dot_general(placing_all, inner_lo, contract_rows, preferred_element_type=jnp.float32)
    d_probs = d_probs.reshape(tok_rows, TOP)
    return (d_tokens, d_probs)


def solution(mesh):
    names = mesh.axis_names
    devices = mesh.devices
    if names != ("dp", "expert"):
        devices = devices.transpose([names.index("dp"), names.index("expert")])
    dp_size = devices.shape[0]
    split = Mesh(
        devices.reshape(GROUP, 2, dp_size // (4 * GROUP), 2, devices.shape[1]), ("l", "sy", "sx", "c", "expert")
    )
    return jax.shard_map(
        shards,
        mesh=split,
        in_specs=(
            P("expert", None),
            P("expert", None),
            P("expert", None),
            P("expert", None),
            P("expert", ("l", "sy", "sx", "c"), None),
            P("expert", ("l", "sy", "sx", "c"), None),
            P("expert", ("l", "sy", "sx", "c"), None),
        ),
        out_specs=(P("expert", ("l", "sy", "sx", "c")), P("expert", None)),
        check_vma=False,
    )
```

```python
import jax
import jax.numpy as jnp
from jax import lax
from jax.sharding import Mesh
from jax.sharding import PartitionSpec as P

FF = 1536
TOP = 8
GROUP = 2


def slot_tables(expert_ids, shard_type, group_size, dest_count, send_rows):
    tok_rows, top_count = expert_ids.shape
    flat_ids = expert_ids.reshape(-1)
    chosen = flat_ids % group_size == shard_type
    target = flat_ids // group_size
    columns = lax.broadcasted_iota(jnp.int32, (flat_ids.shape[0], dest_count), 1)
    matched = jnp.logical_and(chosen[:, None], target[:, None] == columns).astype(jnp.int32)
    ranking = jnp.sum((jnp.cumsum(matched, axis=0) - 1) * matched, axis=1)
    row_index = jnp.where(chosen, target * send_rows + ranking, -1)
    rows_iota = lax.broadcasted_iota(jnp.int32, (dest_count * send_rows, flat_ids.shape[0]), 0)
    placing = (rows_iota == row_index[None, :]).astype(jnp.bfloat16)
    by_token = placing.reshape(dest_count * send_rows, tok_rows, top_count).sum(axis=2)
    return (placing, by_token)


def shards(tokens, cotangent, expert_ids, gate_probs, w_gate, w_up, w_down):
    dest_count = lax.axis_size("expert")
    shard_width = w_gate.shape[1]
    shard_count = FF // shard_width
    group_size = lax.axis_size("l")
    shard_type = lax.axis_index("l")
    part = (lax.axis_index("sy") * lax.axis_size("sx") + lax.axis_index("sx")) * lax.axis_size("c") + lax.axis_index("c")
    core = lax.axis_index("c")
    tok_rows = tokens.shape[0]
    model_width = tokens.shape[1]
    chunk = model_width // shard_count
    out_width = chunk // group_size
    experts_all = group_size * dest_count
    send_rows = (4 * tok_rows * TOP + 3 * experts_all - 1) // (3 * experts_all)
    slots = dest_count * send_rows
    tables = [slot_tables(expert_ids, kind, group_size, dest_count, send_rows) for kind in range(group_size)]
    placing_all = jnp.concatenate([t[0] for t in tables], axis=0)
    by_token_all = jnp.concatenate([t[1] for t in tables], axis=0)
    placing = lax.dynamic_slice_in_dim(placing_all, shard_type * slots, slots, axis=0)
    by_token = lax.dynamic_slice_in_dim(by_token_all, shard_type * slots, slots, axis=0)

    tok_chunk = lax.dynamic_slice_in_dim(tokens, part * chunk, chunk, axis=1)
    cot_chunk = lax.dynamic_slice_in_dim(cotangent, part * chunk, chunk, axis=1)
    both_chunk = jnp.concatenate([tok_chunk, cot_chunk], axis=1)
    rows_sent = jnp.dot(by_token, both_chunk, preferred_element_type=jnp.float32).astype(jnp.bfloat16)
    rows_sent = rows_sent.reshape(dest_count, send_rows, 2 * chunk)
    probs_sent = jnp.dot(
        placing, gate_probs.reshape(-1), preferred_element_type=jnp.float32
    ).astype(jnp.bfloat16)
    probs_row = jnp.pad(probs_sent.reshape(dest_count, 1, send_rows), ((0, 0), (0, 0), (0, 2 * chunk - send_rows)))
    payload = jnp.concatenate([rows_sent, probs_row], axis=1)
    recv = lax.all_to_all(payload, "expert", split_axis=0, concat_axis=0, tiled=True)
    probs_in = recv[:, send_rows, :send_rows].reshape(slots).astype(jnp.float32)
    rows_in = recv[:, :send_rows, :].reshape(slots, 2 * chunk)

    chips = lax.axis_size("sy") * lax.axis_size("sx")
    spread = jnp.broadcast_to(rows_in[None], (chips,) + rows_in.shape)
    same_core = lax.all_to_all(spread, ("sy", "sx"), split_axis=0, concat_axis=0, tiled=True)
    other_core = lax.ppermute(same_core, "c", perm=[(0, 1), (1, 0)])
    by_core = jnp.stack([same_core, other_core, same_core], axis=1)
    gathered = lax.dynamic_slice_in_dim(by_core, core, 2, axis=1).reshape((shard_count,) + rows_in.shape)
    tok_parts = gathered[:, :, :chunk]
    cot_parts = gathered[:, :, chunk:]
    rows_tok = tok_parts.transpose(1, 0, 2).reshape(slots, model_width)
    rows_cot = cot_parts.transpose(1, 0, 2).reshape(slots, model_width)
    gate_shard = w_gate[0]
    up_shard = w_up[0]
    down_shard = w_down[0]
    contract_model = (((1,), (1,)), ((), ()))
    pre_gate = lax.dot_general(rows_tok, gate_shard, contract_model, preferred_element_type=jnp.float32)
    pre_up = lax.dot_general(rows_tok, up_shard, contract_model, preferred_element_type=jnp.float32)
    sigmoid_gate = jax.nn.sigmoid(pre_gate)
    activated = pre_gate * sigmoid_gate
    hidden = (activated * pre_up).astype(jnp.bfloat16)
    outputs = jnp.dot(hidden, down_shard, preferred_element_type=jnp.float32).astype(jnp.bfloat16)
    outputs = lax.optimization_barrier(outputs)
    inner = jnp.sum(
        rows_cot.astype(jnp.float32) * outputs.astype(jnp.float32), axis=1
    ).astype(jnp.bfloat16)
    d_hidden = lax.dot_general(rows_cot, down_shard, contract_model, preferred_element_type=jnp.float32)
    d_hidden = d_hidden * probs_in.reshape(-1, 1)
    d_up = (d_hidden * activated).astype(jnp.bfloat16)
    d_gate = (d_hidden * pre_up * sigmoid_gate * (1.0 + pre_gate * (1.0 - sigmoid_gate))).astype(
        jnp.bfloat16
    )
    d_rows = jnp.dot(d_gate, gate_shard, preferred_element_type=jnp.float32) + jnp.dot(
        d_up, up_shard, preferred_element_type=jnp.float32
    )
    d_rows = d_rows.astype(jnp.bfloat16)
    dp_count = group_size * shard_count
    cores = lax.axis_size("c")
    d_view = d_rows.reshape(slots, dp_count // cores, cores, out_width)
    keep = lax.dynamic_index_in_dim(d_view, core, axis=2, keepdims=False)
    give = lax.dynamic_index_in_dim(d_view, 1 - core, axis=2, keepdims=False)
    swap = [(0, 1), (1, 0)]
    got = lax.ppermute(give, "c", perm=swap)
    inner_peer = lax.ppermute(inner, "c", perm=swap)
    pair_sum = (keep.astype(jnp.float32) + got.astype(jnp.float32)).astype(jnp.bfloat16)
    d_split = pair_sum.transpose(1, 0, 2)
    inner_rows = -(-slots // out_width)
    inner_both = jnp.where(core == 0, jnp.stack([inner, inner_peer]), jnp.stack([inner_peer, inner]))
    inner_block = jnp.pad(inner_both, ((0, 0), (0, inner_rows * out_width - slots)))
    inner_block = inner_block.reshape(1, cores * inner_rows, out_width)
    pad_rows = (-(slots + cores * inner_rows)) % 16
    extra = jnp.concatenate(
        [inner_block, jnp.zeros((1, pad_rows, out_width), jnp.bfloat16)], axis=1
    )
    extra = jnp.broadcast_to(extra, (dp_count // cores,) + extra.shape[1:])
    ex_send = jnp.concatenate([d_split, extra], axis=1)
    ex_recv = lax.all_to_all(ex_send, ("l", "sy", "sx"), split_axis=0, concat_axis=0, tiled=True)
    ex_recv = ex_recv.reshape((group_size, shard_count // cores) + ex_recv.shape[1:]).astype(jnp.float32)
    grads_sum = jnp.sum(ex_recv[:, :, :slots], axis=1)
    inner_parts = ex_recv[:, :, slots:slots + cores * inner_rows].reshape(
        group_size, shard_count // cores, cores, inner_rows * out_width
    )
    inner_sum = jnp.sum(inner_parts, axis=(1, 2))[:, :slots]
    grads_chunk = grads_sum.reshape(group_size, dest_count, send_rows, out_width)
    grads_chunk = grads_chunk.transpose(1, 0, 2, 3).astype(jnp.bfloat16)
    inner_sum = inner_sum.reshape(group_size, dest_count, send_rows).transpose(1, 0, 2)
    inner_hi = inner_sum.astype(jnp.bfloat16)
    inner_lo = (inner_sum - inner_hi.astype(jnp.float32)).astype(jnp.bfloat16)
    inner_pair = jnp.concatenate([inner_hi, inner_lo], axis=2).reshape(dest_count, group_size, 1, 2 * send_rows)
    inner_pair = jnp.pad(inner_pair, ((0, 0), (0, 0), (0, 0), (0, out_width - 2 * send_rows)))
    back_send = jnp.concatenate([grads_chunk, inner_pair], axis=2)
    back = lax.all_to_all(back_send, "expert", split_axis=0, concat_axis=0, tiled=True)

    back = back.transpose(1, 0, 2, 3)
    grads_back = back[:, :, :send_rows, :].reshape(group_size * slots, out_width)
    inner_back = back[:, :, send_rows, :2 * send_rows]
    inner_hi = inner_back[:, :, :send_rows].reshape(group_size * slots)
    inner_lo = inner_back[:, :, send_rows:].reshape(group_size * slots)
    contract_rows = (((0,), (0,)), ((), ()))
    d_tokens = lax.dot_general(
        by_token_all, grads_back, contract_rows, preferred_element_type=jnp.float32
    ).astype(jnp.bfloat16)
    d_probs = lax.dot_general(
        placing_all, inner_hi, contract_rows, preferred_element_type=jnp.float32
    ) + lax.dot_general(placing_all, inner_lo, contract_rows, preferred_element_type=jnp.float32)
    d_probs = d_probs.reshape(tok_rows, TOP)
    return (d_tokens, d_probs)


def solution(mesh):
    names = mesh.axis_names
    devices = mesh.devices
    if names != ("dp", "expert"):
        devices = devices.transpose([names.index("dp"), names.index("expert")])
    dp_size = devices.shape[0]
    split = Mesh(
        devices.reshape(GROUP, 2, dp_size // (4 * GROUP), 2, devices.shape[1]), ("l", "sy", "sx", "c", "expert")
    )
    return jax.shard_map(
        shards,
        mesh=split,
        in_specs=(
            P("expert", None),
            P("expert", None),
            P("expert", None),
            P("expert", None),
            P("expert", ("l", "sy", "sx", "c"), None),
            P("expert", ("l", "sy", "sx", "c"), None),
            P("expert", ("l", "sy", "sx", "c"), None),
        ),
        out_specs=(P("expert", ("l", "sy", "sx", "c")), P("expert", None)),
        check_vma=False,
    )
```

```python
import jax
import jax.numpy as jnp
from jax import lax
from jax.sharding import Mesh
from jax.sharding import PartitionSpec as P

FF = 1536
TOP = 8
GROUP = 2


def slot_tables(expert_ids, shard_type, group_size, dest_count, send_rows):
    tok_rows, top_count = expert_ids.shape
    flat_ids = expert_ids.reshape(-1)
    chosen = flat_ids % group_size == shard_type
    target = flat_ids // group_size
    columns = lax.broadcasted_iota(jnp.int32, (flat_ids.shape[0], dest_count), 1)
    matched = jnp.logical_and(chosen[:, None], target[:, None] == columns).astype(jnp.int32)
    ranking = jnp.sum((jnp.cumsum(matched, axis=0) - 1) * matched, axis=1)
    row_index = jnp.where(chosen, target * send_rows + ranking, -1)
    rows_iota = lax.broadcasted_iota(jnp.int32, (dest_count * send_rows, flat_ids.shape[0]), 0)
    placing = (rows_iota == row_index[None, :]).astype(jnp.bfloat16)
    by_token = placing.reshape(dest_count * send_rows, tok_rows, top_count).sum(axis=2)
    return (placing, by_token)


def shards(tokens, cotangent, expert_ids, gate_probs, w_gate, w_up, w_down):
    dest_count = lax.axis_size("expert")
    shard_width = w_gate.shape[1]
    shard_count = FF // shard_width
    group_size = lax.axis_size("l")
    shard_type = lax.axis_index("l")
    part = (lax.axis_index("sy") * lax.axis_size("sx") + lax.axis_index("sx")) * lax.axis_size("c") + lax.axis_index("c")
    core = lax.axis_index("c")
    tok_rows = tokens.shape[0]
    model_width = tokens.shape[1]
    chunk = model_width // shard_count
    out_width = chunk // group_size
    experts_all = group_size * dest_count
    send_rows = (4 * tok_rows * TOP + 3 * experts_all - 1) // (3 * experts_all)
    slots = dest_count * send_rows
    tables = [slot_tables(expert_ids, kind, group_size, dest_count, send_rows) for kind in range(group_size)]
    placing_all = jnp.concatenate([t[0] for t in tables], axis=0)
    by_token_all = jnp.concatenate([t[1] for t in tables], axis=0)
    placing = lax.dynamic_slice_in_dim(placing_all, shard_type * slots, slots, axis=0)
    by_token = lax.dynamic_slice_in_dim(by_token_all, shard_type * slots, slots, axis=0)

    tok_chunk = lax.dynamic_slice_in_dim(tokens, part * chunk, chunk, axis=1)
    cot_chunk = lax.dynamic_slice_in_dim(cotangent, part * chunk, chunk, axis=1)
    both_chunk = jnp.concatenate([tok_chunk, cot_chunk], axis=1)
    rows_sent = jnp.dot(by_token, both_chunk, preferred_element_type=jnp.float32).astype(jnp.bfloat16)
    rows_sent = rows_sent.reshape(dest_count, send_rows, 2 * chunk)
    probs_sent = jnp.dot(
        placing, gate_probs.reshape(-1), preferred_element_type=jnp.float32
    ).astype(jnp.bfloat16)
    probs_row = jnp.pad(probs_sent.reshape(dest_count, 1, send_rows), ((0, 0), (0, 0), (0, 2 * chunk - send_rows)))
    payload = jnp.concatenate([rows_sent, probs_row], axis=1)
    recv = lax.all_to_all(payload, "expert", split_axis=0, concat_axis=0, tiled=True)
    probs_in = recv[:, send_rows, :send_rows].reshape(slots).astype(jnp.float32)
    rows_in = recv[:, :send_rows, :].reshape(slots, 2 * chunk)

    chips = lax.axis_size("sy") * lax.axis_size("sx")
    spread = jnp.broadcast_to(rows_in[None], (chips,) + rows_in.shape)
    same_core = lax.all_to_all(spread, ("sy", "sx"), split_axis=0, concat_axis=0, tiled=True)
    other_core = lax.ppermute(same_core, "c", perm=[(0, 1), (1, 0)])
    by_core = jnp.stack([same_core, other_core, same_core], axis=1)
    gathered = lax.dynamic_slice_in_dim(by_core, core, 2, axis=1).reshape((shard_count,) + rows_in.shape)
    tok_parts = gathered[:, :, :chunk]
    cot_parts = gathered[:, :, chunk:]
    rows_tok = tok_parts.transpose(1, 0, 2).reshape(slots, model_width)
    rows_cot = cot_parts.transpose(1, 0, 2).reshape(slots, model_width)
    gate_shard = w_gate[0]
    up_shard = w_up[0]
    down_shard = w_down[0]
    contract_model = (((1,), (1,)), ((), ()))
    pre_gate = lax.dot_general(rows_tok, gate_shard, contract_model, preferred_element_type=jnp.float32)
    pre_up = lax.dot_general(rows_tok, up_shard, contract_model, preferred_element_type=jnp.float32)
    sigmoid_gate = jax.nn.sigmoid(pre_gate)
    activated = pre_gate * sigmoid_gate
    hidden = (activated * pre_up).astype(jnp.bfloat16)
    outputs = jnp.dot(hidden, down_shard, preferred_element_type=jnp.float32).astype(jnp.bfloat16)
    outputs = lax.optimization_barrier(outputs)
    inner = jnp.sum(
        rows_cot.astype(jnp.float32) * outputs.astype(jnp.float32), axis=1
    ).astype(jnp.bfloat16)
    d_hidden = lax.dot_general(rows_cot, down_shard, contract_model, preferred_element_type=jnp.float32)
    d_hidden = d_hidden * probs_in.reshape(-1, 1)
    d_up = (d_hidden * activated).astype(jnp.bfloat16)
    d_gate = (d_hidden * pre_up * sigmoid_gate * (1.0 + pre_gate * (1.0 - sigmoid_gate))).astype(
        jnp.bfloat16
    )
    dp_count = group_size * shard_count
    cores = lax.axis_size("c")
    col_view = (gate_shard.shape[0], dp_count // cores, cores, out_width)

    def columns(weight, which):
        return lax.dynamic_index_in_dim(weight.reshape(col_view), which, axis=2, keepdims=False)

    def part_rows(which):
        rows = jnp.einsum(
            "ru,ukf->krf", d_gate, columns(gate_shard, which), preferred_element_type=jnp.float32
        ) + jnp.einsum("ru,ukf->krf", d_up, columns(up_shard, which), preferred_element_type=jnp.float32)
        return rows.astype(jnp.bfloat16)

    keep = part_rows(core)
    give = part_rows(1 - core)
    swap = [(0, 1), (1, 0)]
    got = lax.ppermute(give, "c", perm=swap)
    inner_peer = lax.ppermute(inner, "c", perm=swap)
    d_split = (keep.astype(jnp.float32) + got.astype(jnp.float32)).astype(jnp.bfloat16)
    inner_rows = -(-slots // out_width)
    inner_both = jnp.where(core == 0, jnp.stack([inner, inner_peer]), jnp.stack([inner_peer, inner]))
    inner_block = jnp.pad(inner_both, ((0, 0), (0, inner_rows * out_width - slots)))
    inner_block = inner_block.reshape(1, cores * inner_rows, out_width)
    pad_rows = (-(slots + cores * inner_rows)) % 16
    extra = jnp.concatenate(
        [inner_block, jnp.zeros((1, pad_rows, out_width), jnp.bfloat16)], axis=1
    )
    extra = jnp.broadcast_to(extra, (dp_count // cores,) + extra.shape[1:])
    ex_send = jnp.concatenate([d_split, extra], axis=1)
    ex_recv = lax.all_to_all(ex_send, ("l", "sy", "sx"), split_axis=0, concat_axis=0, tiled=True)
    ex_recv = ex_recv.reshape((group_size, shard_count // cores) + ex_recv.shape[1:]).astype(jnp.float32)
    grads_sum = jnp.sum(ex_recv[:, :, :slots], axis=1)
    inner_parts = ex_recv[:, :, slots:slots + cores * inner_rows].reshape(
        group_size, shard_count // cores, cores, inner_rows * out_width
    )
    inner_sum = jnp.sum(inner_parts, axis=(1, 2))[:, :slots]
    grads_chunk = grads_sum.reshape(group_size, dest_count, send_rows, out_width)
    grads_chunk = grads_chunk.transpose(1, 0, 2, 3).astype(jnp.bfloat16)
    inner_sum = inner_sum.reshape(group_size, dest_count, send_rows).transpose(1, 0, 2)
    inner_hi = inner_sum.astype(jnp.bfloat16)
    inner_lo = (inner_sum - inner_hi.astype(jnp.float32)).astype(jnp.bfloat16)
    inner_pair = jnp.concatenate([inner_hi, inner_lo], axis=2).reshape(dest_count, group_size, 1, 2 * send_rows)
    inner_pair = jnp.pad(inner_pair, ((0, 0), (0, 0), (0, 0), (0, out_width - 2 * send_rows)))
    back_send = jnp.concatenate([grads_chunk, inner_pair], axis=2)
    back = lax.all_to_all(back_send, "expert", split_axis=0, concat_axis=0, tiled=True)

    back = back.transpose(1, 0, 2, 3)
    grads_back = back[:, :, :send_rows, :].reshape(group_size * slots, out_width)
    inner_back = back[:, :, send_rows, :2 * send_rows]
    inner_hi = inner_back[:, :, :send_rows].reshape(group_size * slots)
    inner_lo = inner_back[:, :, send_rows:].reshape(group_size * slots)
    contract_rows = (((0,), (0,)), ((), ()))
    d_tokens = lax.dot_general(
        by_token_all, grads_back, contract_rows, preferred_element_type=jnp.float32
    ).astype(jnp.bfloat16)
    d_probs = lax.dot_general(
        placing_all, inner_hi, contract_rows, preferred_element_type=jnp.float32
    ) + lax.dot_general(placing_all, inner_lo, contract_rows, preferred_element_type=jnp.float32)
    d_probs = d_probs.reshape(tok_rows, TOP)
    return (d_tokens, d_probs)


def solution(mesh):
    names = mesh.axis_names
    devices = mesh.devices
    if names != ("dp", "expert"):
        devices = devices.transpose([names.index("dp"), names.index("expert")])
    dp_size = devices.shape[0]
    split = Mesh(
        devices.reshape(GROUP, 2, dp_size // (4 * GROUP), 2, devices.shape[1]), ("l", "sy", "sx", "c", "expert")
    )
    return jax.shard_map(
        shards,
        mesh=split,
        in_specs=(
            P("expert", None),
            P("expert", None),
            P("expert", None),
            P("expert", None),
            P("expert", ("l", "sy", "sx", "c"), None),
            P("expert", ("l", "sy", "sx", "c"), None),
            P("expert", ("l", "sy", "sx", "c"), None),
        ),
        out_specs=(P("expert", ("l", "sy", "sx", "c")), P("expert", None)),
        check_vma=False,
    )
```

```python
import jax
import jax.numpy as jnp
from jax import lax
from jax.sharding import Mesh
from jax.sharding import PartitionSpec as P

FF = 1536
TOP = 8
GROUP = 2


def slot_tables(expert_ids, shard_type, group_size, dest_count, send_rows):
    tok_rows, top_count = expert_ids.shape
    flat_ids = expert_ids.reshape(-1)
    chosen = flat_ids % group_size == shard_type
    target = flat_ids // group_size
    columns = lax.broadcasted_iota(jnp.int32, (flat_ids.shape[0], dest_count), 1)
    matched = jnp.logical_and(chosen[:, None], target[:, None] == columns).astype(jnp.int32)
    ranking = jnp.sum((jnp.cumsum(matched, axis=0) - 1) * matched, axis=1)
    row_index = jnp.where(chosen, target * send_rows + ranking, -1)
    rows_iota = lax.broadcasted_iota(jnp.int32, (dest_count * send_rows, flat_ids.shape[0]), 0)
    placing = (rows_iota == row_index[None, :]).astype(jnp.bfloat16)
    by_token = placing.reshape(dest_count * send_rows, tok_rows, top_count).sum(axis=2)
    return (placing, by_token)


def shards(tokens, cotangent, expert_ids, gate_probs, w_gate, w_up, w_down):
    dest_count = lax.axis_size("expert")
    shard_width = w_gate.shape[1]
    shard_count = FF // shard_width
    group_size = lax.axis_size("l")
    shard_type = lax.axis_index("l")
    part = (lax.axis_index("sy") * lax.axis_size("sx") + lax.axis_index("sx")) * lax.axis_size("c") + lax.axis_index("c")
    core = lax.axis_index("c")
    tok_rows = tokens.shape[0]
    model_width = tokens.shape[1]
    chunk = model_width // shard_count
    out_width = chunk // group_size
    experts_all = group_size * dest_count
    send_rows = (4 * tok_rows * TOP + 3 * experts_all - 1) // (3 * experts_all)
    slots = dest_count * send_rows
    tables = [slot_tables(expert_ids, kind, group_size, dest_count, send_rows) for kind in range(group_size)]
    placing_all = jnp.concatenate([t[0] for t in tables], axis=0)
    by_token_all = jnp.concatenate([t[1] for t in tables], axis=0)
    placing = lax.dynamic_slice_in_dim(placing_all, shard_type * slots, slots, axis=0)
    by_token = lax.dynamic_slice_in_dim(by_token_all, shard_type * slots, slots, axis=0)

    tok_chunk = lax.dynamic_slice_in_dim(tokens, part * chunk, chunk, axis=1)
    cot_chunk = lax.dynamic_slice_in_dim(cotangent, part * chunk, chunk, axis=1)
    both_chunk = jnp.concatenate([tok_chunk, cot_chunk], axis=1)
    rows_sent = jnp.dot(by_token, both_chunk, preferred_element_type=jnp.float32).astype(jnp.bfloat16)
    rows_sent = rows_sent.reshape(dest_count, send_rows, 2 * chunk)
    probs_sent = jnp.dot(
        placing, gate_probs.reshape(-1), preferred_element_type=jnp.float32
    ).astype(jnp.bfloat16)
    probs_row = jnp.pad(probs_sent.reshape(dest_count, 1, send_rows), ((0, 0), (0, 0), (0, 2 * chunk - send_rows)))
    payload = jnp.concatenate([rows_sent, probs_row], axis=1)
    recv = lax.all_to_all(payload, "expert", split_axis=0, concat_axis=0, tiled=True)
    probs_in = recv[:, send_rows, :send_rows].reshape(slots).astype(jnp.float32)
    rows_in = recv[:, :send_rows, :].reshape(slots, 2 * chunk)

    chips = lax.axis_size("sy") * lax.axis_size("sx")
    spread = jnp.broadcast_to(rows_in[None], (chips,) + rows_in.shape)
    same_core = lax.all_to_all(spread, ("sy", "sx"), split_axis=0, concat_axis=0, tiled=True)
    other_core = lax.ppermute(same_core, "c", perm=[(0, 1), (1, 0)])
    by_core = jnp.stack([same_core, other_core, same_core], axis=1)
    gathered = lax.dynamic_slice_in_dim(by_core, core, 2, axis=1).reshape((shard_count,) + rows_in.shape)
    tok_parts = gathered[:, :, :chunk]
    cot_parts = gathered[:, :, chunk:]
    rows_tok = tok_parts.transpose(1, 0, 2).reshape(slots, model_width)
    rows_cot = cot_parts.transpose(1, 0, 2).reshape(slots, model_width)
    gate_shard = w_gate[0]
    up_shard = w_up[0]
    down_shard = w_down[0]
    contract_model = (((1,), (1,)), ((), ()))
    pre_gate = lax.dot_general(rows_tok, gate_shard, contract_model, preferred_element_type=jnp.float32)
    pre_up = lax.dot_general(rows_tok, up_shard, contract_model, preferred_element_type=jnp.float32)
    sigmoid_gate = jax.nn.sigmoid(pre_gate)
    activated = pre_gate * sigmoid_gate
    hidden = (activated * pre_up).astype(jnp.bfloat16)
    d_down = lax.dot_general(rows_cot, down_shard, contract_model, preferred_element_type=jnp.float32)
    inner = jnp.sum(hidden.astype(jnp.float32) * d_down, axis=1).astype(jnp.bfloat16)
    d_hidden = d_down * probs_in.reshape(-1, 1)
    d_up = (d_hidden * activated).astype(jnp.bfloat16)
    d_gate = (d_hidden * pre_up * sigmoid_gate * (1.0 + pre_gate * (1.0 - sigmoid_gate))).astype(
        jnp.bfloat16
    )
    d_rows = jnp.dot(d_gate, gate_shard, preferred_element_type=jnp.float32) + jnp.dot(
        d_up, up_shard, preferred_element_type=jnp.float32
    )
    d_rows = d_rows.astype(jnp.bfloat16)
    dp_count = group_size * shard_count
    d_split = d_rows.reshape(slots, dp_count, out_width).transpose(1, 0, 2)
    inner_rows = -(-slots // out_width)
    pad_rows = (-(slots + inner_rows)) % 16
    inner_block = jnp.pad(inner, (0, inner_rows * out_width - slots)).reshape(1, inner_rows, out_width)
    extra = jnp.concatenate(
        [inner_block, jnp.zeros((1, pad_rows, out_width), jnp.bfloat16)], axis=1
    )
    extra = jnp.broadcast_to(extra, (dp_count,) + extra.shape[1:])
    ex_send = jnp.concatenate([d_split, extra], axis=1)
    ex_recv = lax.all_to_all(ex_send, ("l", "sy", "sx", "c"), split_axis=0, concat_axis=0, tiled=True)
    ex_recv = ex_recv.reshape((group_size, shard_count) + ex_recv.shape[1:])
    summed = jnp.sum(ex_recv.astype(jnp.float32), axis=1)
    grads_chunk = summed[:, :slots].reshape(group_size, dest_count, send_rows, out_width)
    grads_chunk = grads_chunk.transpose(1, 0, 2, 3).astype(jnp.bfloat16)
    inner_sum = summed[:, slots:slots + inner_rows].reshape(group_size, inner_rows * out_width)
    inner_sum = inner_sum[:, :slots].reshape(group_size, dest_count, send_rows).transpose(1, 0, 2)
    inner_hi = inner_sum.astype(jnp.bfloat16)
    inner_lo = (inner_sum - inner_hi.astype(jnp.float32)).astype(jnp.bfloat16)
    inner_pair = jnp.concatenate([inner_hi, inner_lo], axis=2).reshape(dest_count, group_size, 1, 2 * send_rows)
    inner_pair = jnp.pad(inner_pair, ((0, 0), (0, 0), (0, 0), (0, out_width - 2 * send_rows)))
    back_send = jnp.concatenate([grads_chunk, inner_pair], axis=2)
    back = lax.all_to_all(back_send, "expert", split_axis=0, concat_axis=0, tiled=True)

    back = back.transpose(1, 0, 2, 3)
    grads_back = back[:, :, :send_rows, :].reshape(group_size * slots, out_width)
    inner_back = back[:, :, send_rows, :2 * send_rows]
    inner_hi = inner_back[:, :, :send_rows].reshape(group_size * slots)
    inner_lo = inner_back[:, :, send_rows:].reshape(group_size * slots)
    contract_rows = (((0,), (0,)), ((), ()))
    d_tokens = lax.dot_general(
        by_token_all, grads_back, contract_rows, preferred_element_type=jnp.float32
    ).astype(jnp.bfloat16)
    d_probs = lax.dot_general(
        placing_all, inner_hi, contract_rows, preferred_element_type=jnp.float32
    ) + lax.dot_general(placing_all, inner_lo, contract_rows, preferred_element_type=jnp.float32)
    d_probs = d_probs.reshape(tok_rows, TOP)
    return (d_tokens, d_probs)


def solution(mesh):
    names = mesh.axis_names
    devices = mesh.devices
    if names != ("dp", "expert"):
        devices = devices.transpose([names.index("dp"), names.index("expert")])
    dp_size = devices.shape[0]
    split = Mesh(
        devices.reshape(GROUP, 2, dp_size // (4 * GROUP), 2, devices.shape[1]), ("l", "sy", "sx", "c", "expert")
    )
    return jax.shard_map(
        shards,
        mesh=split,
        in_specs=(
            P("expert", None),
            P("expert", None),
            P("expert", None),
            P("expert", None),
            P("expert", ("l", "sy", "sx", "c"), None),
            P("expert", ("l", "sy", "sx", "c"), None),
            P("expert", ("l", "sy", "sx", "c"), None),
        ),
        out_specs=(P("expert", ("l", "sy", "sx", "c")), P("expert", None)),
        check_vma=False,
    )
```

```python
import jax
import jax.numpy as jnp
from jax import lax
from jax.sharding import Mesh
from jax.sharding import PartitionSpec as P

FF = 1536
TOP = 8
GROUP = 2


def slot_tables(expert_ids, shard_type, group_size, dest_count, send_rows):
    tok_rows, top_count = expert_ids.shape
    flat_ids = expert_ids.reshape(-1)
    chosen = flat_ids % group_size == shard_type
    target = flat_ids // group_size
    columns = lax.broadcasted_iota(jnp.int32, (flat_ids.shape[0], dest_count), 1)
    matched = jnp.logical_and(chosen[:, None], target[:, None] == columns).astype(jnp.int32)
    ranking = jnp.sum((jnp.cumsum(matched, axis=0) - 1) * matched, axis=1)
    row_index = jnp.where(chosen, target * send_rows + ranking, -1)
    rows_iota = lax.broadcasted_iota(jnp.int32, (dest_count * send_rows, flat_ids.shape[0]), 0)
    placing = (rows_iota == row_index[None, :]).astype(jnp.bfloat16)
    by_token = placing.reshape(dest_count * send_rows, tok_rows, top_count).sum(axis=2)
    return (placing, by_token)


def shards(tokens, cotangent, expert_ids, gate_probs, w_gate, w_up, w_down):
    dest_count = lax.axis_size("expert")
    shard_width = w_gate.shape[1]
    shard_count = FF // shard_width
    group_size = lax.axis_size("l")
    shard_type = lax.axis_index("l")
    part = (lax.axis_index("sy") * lax.axis_size("sx") + lax.axis_index("sx")) * lax.axis_size("c") + lax.axis_index("c")
    core = lax.axis_index("c")
    tok_rows = tokens.shape[0]
    model_width = tokens.shape[1]
    chunk = model_width // shard_count
    out_width = chunk // group_size
    experts_all = group_size * dest_count
    send_rows = (4 * tok_rows * TOP + 3 * experts_all - 1) // (3 * experts_all)
    slots = dest_count * send_rows
    tables = [slot_tables(expert_ids, kind, group_size, dest_count, send_rows) for kind in range(group_size)]
    placing_all = jnp.concatenate([t[0] for t in tables], axis=0)
    by_token_all = jnp.concatenate([t[1] for t in tables], axis=0)
    placing = lax.dynamic_slice_in_dim(placing_all, shard_type * slots, slots, axis=0)
    by_token = lax.dynamic_slice_in_dim(by_token_all, shard_type * slots, slots, axis=0)

    tok_chunk = lax.dynamic_slice_in_dim(tokens, part * chunk, chunk, axis=1)
    cot_chunk = lax.dynamic_slice_in_dim(cotangent, part * chunk, chunk, axis=1)
    both_chunk = jnp.concatenate([tok_chunk, cot_chunk], axis=1)
    rows_sent = jnp.dot(by_token, both_chunk, preferred_element_type=jnp.float32).astype(jnp.bfloat16)
    row_words = send_rows * 2 * chunk
    rows_sent = rows_sent.reshape(dest_count, row_words)
    probs_sent = jnp.dot(
        placing, gate_probs.reshape(-1), preferred_element_type=jnp.float32
    ).astype(jnp.bfloat16)
    fwd_pad = (-(row_words + send_rows)) % 128
    payload = jnp.concatenate(
        [rows_sent, probs_sent.reshape(dest_count, send_rows), jnp.zeros((dest_count, fwd_pad), jnp.bfloat16)],
        axis=1,
    )
    recv = lax.all_to_all(payload, "expert", split_axis=0, concat_axis=0, tiled=True)
    probs_in = recv[:, row_words:row_words + send_rows].reshape(slots).astype(jnp.float32)
    rows_in = recv[:, :row_words].reshape(slots, 2 * chunk)

    chips = lax.axis_size("sy") * lax.axis_size("sx")
    spread = jnp.broadcast_to(rows_in[None], (chips,) + rows_in.shape)
    same_core = lax.all_to_all(spread, ("sy", "sx"), split_axis=0, concat_axis=0, tiled=True)
    other_core = lax.ppermute(same_core, "c", perm=[(0, 1), (1, 0)])
    by_core = jnp.stack([same_core, other_core, same_core], axis=1)
    gathered = lax.dynamic_slice_in_dim(by_core, core, 2, axis=1).reshape((shard_count,) + rows_in.shape)
    tok_parts = gathered[:, :, :chunk]
    cot_parts = gathered[:, :, chunk:]
    rows_tok = tok_parts.transpose(1, 0, 2).reshape(slots, model_width)
    rows_cot = cot_parts.transpose(1, 0, 2).reshape(slots, model_width)
    gate_shard = w_gate[0]
    up_shard = w_up[0]
    down_shard = w_down[0]
    contract_model = (((1,), (1,)), ((), ()))
    pre_gate = lax.dot_general(rows_tok, gate_shard, contract_model, preferred_element_type=jnp.float32)
    pre_up = lax.dot_general(rows_tok, up_shard, contract_model, preferred_element_type=jnp.float32)
    sigmoid_gate = jax.nn.sigmoid(pre_gate)
    activated = pre_gate * sigmoid_gate
    hidden = (activated * pre_up).astype(jnp.bfloat16)
    outputs = jnp.dot(hidden, down_shard, preferred_element_type=jnp.float32).astype(jnp.bfloat16)
    outputs = lax.optimization_barrier(outputs)
    inner = jnp.sum(
        rows_cot.astype(jnp.float32) * outputs.astype(jnp.float32), axis=1
    ).astype(jnp.bfloat16)
    d_hidden = lax.dot_general(rows_cot, down_shard, contract_model, preferred_element_type=jnp.float32)
    d_hidden = d_hidden * probs_in.reshape(-1, 1)
    d_up = (d_hidden * activated).astype(jnp.bfloat16)
    d_gate = (d_hidden * pre_up * sigmoid_gate * (1.0 + pre_gate * (1.0 - sigmoid_gate))).astype(
        jnp.bfloat16
    )
    d_rows = jnp.dot(d_gate, gate_shard, preferred_element_type=jnp.float32) + jnp.dot(
        d_up, up_shard, preferred_element_type=jnp.float32
    )
    d_rows = d_rows.astype(jnp.bfloat16)
    dp_count = group_size * shard_count
    d_split = d_rows.reshape(slots, dp_count, out_width).transpose(1, 0, 2)
    inner_rows = -(-slots // out_width)
    pad_rows = (-(slots + inner_rows)) % 16
    inner_block = jnp.pad(inner, (0, inner_rows * out_width - slots)).reshape(1, inner_rows, out_width)
    extra = jnp.concatenate(
        [inner_block, jnp.zeros((1, pad_rows, out_width), jnp.bfloat16)], axis=1
    )
    extra = jnp.broadcast_to(extra, (dp_count,) + extra.shape[1:])
    ex_send = jnp.concatenate([d_split, extra], axis=1)
    ex_recv = lax.all_to_all(ex_send, ("l", "sy", "sx", "c"), split_axis=0, concat_axis=0, tiled=True)
    ex_recv = ex_recv.reshape((group_size, shard_count) + ex_recv.shape[1:])
    summed = jnp.sum(ex_recv.astype(jnp.float32), axis=1)
    grads_chunk = summed[:, :slots].reshape(group_size, dest_count, send_rows, out_width)
    grads_chunk = grads_chunk.transpose(1, 0, 2, 3).astype(jnp.bfloat16)
    inner_sum = summed[:, slots:slots + inner_rows].reshape(group_size, inner_rows * out_width)
    inner_sum = inner_sum[:, :slots].reshape(group_size, dest_count, send_rows).transpose(1, 0, 2)
    inner_hi = inner_sum.astype(jnp.bfloat16)
    inner_lo = (inner_sum - inner_hi.astype(jnp.float32)).astype(jnp.bfloat16)
    grad_words = group_size * send_rows * out_width
    inner_pair = jnp.stack([inner_hi, inner_lo], axis=1).reshape(dest_count, 2 * group_size * send_rows)
    back_pad = (-(grad_words + 2 * group_size * send_rows)) % 128
    back_send = jnp.concatenate(
        [grads_chunk.reshape(dest_count, grad_words), inner_pair, jnp.zeros((dest_count, back_pad), jnp.bfloat16)],
        axis=1,
    )
    back = lax.all_to_all(back_send, "expert", split_axis=0, concat_axis=0, tiled=True)

    grads_back = back[:, :grad_words].reshape(dest_count, group_size, send_rows, out_width)
    grads_back = grads_back.transpose(1, 0, 2, 3).reshape(group_size * slots, out_width)
    inner_back = back[:, grad_words:grad_words + 2 * group_size * send_rows]
    inner_back = inner_back.reshape(dest_count, 2, group_size, send_rows).transpose(1, 2, 0, 3)
    inner_hi = inner_back[0].reshape(group_size * slots)
    inner_lo = inner_back[1].reshape(group_size * slots)
    contract_rows = (((0,), (0,)), ((), ()))
    d_tokens = lax.dot_general(
        by_token_all, grads_back, contract_rows, preferred_element_type=jnp.float32
    ).astype(jnp.bfloat16)
    d_probs = lax.dot_general(
        placing_all, inner_hi, contract_rows, preferred_element_type=jnp.float32
    ) + lax.dot_general(placing_all, inner_lo, contract_rows, preferred_element_type=jnp.float32)
    d_probs = d_probs.reshape(tok_rows, TOP)
    return (d_tokens, d_probs)


def solution(mesh):
    names = mesh.axis_names
    devices = mesh.devices
    if names != ("dp", "expert"):
        devices = devices.transpose([names.index("dp"), names.index("expert")])
    dp_size = devices.shape[0]
    split = Mesh(
        devices.reshape(GROUP, 2, dp_size // (4 * GROUP), 2, devices.shape[1]), ("l", "sy", "sx", "c", "expert")
    )
    return jax.shard_map(
        shards,
        mesh=split,
        in_specs=(
            P("expert", None),
            P("expert", None),
            P("expert", None),
            P("expert", None),
            P("expert", ("l", "sy", "sx", "c"), None),
            P("expert", ("l", "sy", "sx", "c"), None),
            P("expert", ("l", "sy", "sx", "c"), None),
        ),
        out_specs=(P("expert", ("l", "sy", "sx", "c")), P("expert", None)),
        check_vma=False,
    )
```

```python
import jax
import jax.numpy as jnp
from jax import lax
from jax.sharding import Mesh
from jax.sharding import PartitionSpec as P

FF = 1536
TOP = 8
GROUP = 2


def slot_tables(expert_ids, shard_type, group_size, dest_count, send_rows):
    tok_rows, top_count = expert_ids.shape
    flat_ids = expert_ids.reshape(-1)
    chosen = flat_ids % group_size == shard_type
    target = flat_ids // group_size
    columns = lax.broadcasted_iota(jnp.int32, (flat_ids.shape[0], dest_count), 1)
    matched = jnp.logical_and(chosen[:, None], target[:, None] == columns).astype(jnp.int32)
    ranking = jnp.sum((jnp.cumsum(matched, axis=0) - 1) * matched, axis=1)
    row_index = jnp.where(chosen, target * send_rows + ranking, -1)
    rows_iota = lax.broadcasted_iota(jnp.int32, (dest_count * send_rows, flat_ids.shape[0]), 0)
    placing = (rows_iota == row_index[None, :]).astype(jnp.bfloat16)
    by_token = placing.reshape(dest_count * send_rows, tok_rows, top_count).sum(axis=2)
    return (placing, by_token)


def shards(tokens, cotangent, expert_ids, gate_probs, w_gate, w_up, w_down):
    dest_count = lax.axis_size("expert")
    shard_width = w_gate.shape[1]
    shard_count = FF // shard_width
    group_size = lax.axis_size("l")
    shard_type = lax.axis_index("l")
    part = (lax.axis_index("sy") * lax.axis_size("sx") + lax.axis_index("sx")) * lax.axis_size("c") + lax.axis_index("c")
    core = lax.axis_index("c")
    tok_rows = tokens.shape[0]
    model_width = tokens.shape[1]
    chunk = model_width // shard_count
    out_width = chunk // group_size
    experts_all = group_size * dest_count
    send_rows = (4 * tok_rows * TOP + 3 * experts_all - 1) // (3 * experts_all)
    slots = dest_count * send_rows
    tables = [slot_tables(expert_ids, kind, group_size, dest_count, send_rows) for kind in range(group_size)]
    placing_all = jnp.concatenate([t[0] for t in tables], axis=0)
    by_token_all = jnp.concatenate([t[1] for t in tables], axis=0)
    placing = lax.dynamic_slice_in_dim(placing_all, shard_type * slots, slots, axis=0)
    by_token = lax.dynamic_slice_in_dim(by_token_all, shard_type * slots, slots, axis=0)

    tok_chunk = lax.dynamic_slice_in_dim(tokens, part * chunk, chunk, axis=1)
    cot_chunk = lax.dynamic_slice_in_dim(cotangent, part * chunk, chunk, axis=1)
    both_chunk = jnp.concatenate([tok_chunk, cot_chunk], axis=1)
    rows_sent = jnp.dot(by_token, both_chunk, preferred_element_type=jnp.float32).astype(jnp.bfloat16)
    rows_sent = rows_sent.reshape(dest_count, send_rows, 2 * chunk)
    probs_sent = jnp.dot(
        placing, gate_probs.reshape(-1), preferred_element_type=jnp.float32
    ).astype(jnp.bfloat16)
    probs_row = jnp.pad(probs_sent.reshape(dest_count, 1, send_rows), ((0, 0), (0, 0), (0, 2 * chunk - send_rows)))
    payload = jnp.concatenate([rows_sent, probs_row], axis=1)
    recv = lax.all_to_all(payload, "expert", split_axis=0, concat_axis=0, tiled=True)
    probs_in = recv[:, send_rows, :send_rows].reshape(slots).astype(jnp.float32)
    rows_in = recv[:, :send_rows, :].reshape(slots, 2 * chunk)

    chips = lax.axis_size("sy") * lax.axis_size("sx")
    spread = jnp.broadcast_to(rows_in[None], (chips,) + rows_in.shape)
    same_core = lax.all_to_all(spread, ("sy", "sx"), split_axis=0, concat_axis=0, tiled=True)
    other_core = lax.ppermute(same_core, "c", perm=[(0, 1), (1, 0)])
    cores = lax.axis_size("c")

    def place(rows, block, which):
        return lax.dynamic_update_slice(rows, block.transpose(1, 0, 2)[:, :, None, :], (0, 0, which, 0))

    empty = jnp.zeros((slots, chips, cores, chunk), jnp.bfloat16)
    rows_tok = place(empty, same_core[:, :, :chunk], core)
    rows_cot = place(empty, same_core[:, :, chunk:], core)
    rows_tok = place(rows_tok, other_core[:, :, :chunk], 1 - core).reshape(slots, model_width)
    rows_cot = place(rows_cot, other_core[:, :, chunk:], 1 - core).reshape(slots, model_width)
    gate_shard = w_gate[0]
    up_shard = w_up[0]
    down_shard = w_down[0]
    contract_model = (((1,), (1,)), ((), ()))
    pre_gate = lax.dot_general(rows_tok, gate_shard, contract_model, preferred_element_type=jnp.float32)
    pre_up = lax.dot_general(rows_tok, up_shard, contract_model, preferred_element_type=jnp.float32)
    sigmoid_gate = jax.nn.sigmoid(pre_gate)
    activated = pre_gate * sigmoid_gate
    hidden = (activated * pre_up).astype(jnp.bfloat16)
    outputs = jnp.dot(hidden, down_shard, preferred_element_type=jnp.float32).astype(jnp.bfloat16)
    outputs = lax.optimization_barrier(outputs)
    inner = jnp.sum(
        rows_cot.astype(jnp.float32) * outputs.astype(jnp.float32), axis=1
    ).astype(jnp.bfloat16)
    d_hidden = lax.dot_general(rows_cot, down_shard, contract_model, preferred_element_type=jnp.float32)
    d_hidden = d_hidden * probs_in.reshape(-1, 1)
    d_up = (d_hidden * activated).astype(jnp.bfloat16)
    d_gate = (d_hidden * pre_up * sigmoid_gate * (1.0 + pre_gate * (1.0 - sigmoid_gate))).astype(
        jnp.bfloat16
    )
    d_rows = jnp.dot(d_gate, gate_shard, preferred_element_type=jnp.float32) + jnp.dot(
        d_up, up_shard, preferred_element_type=jnp.float32
    )
    d_rows = d_rows.astype(jnp.bfloat16)
    dp_count = group_size * shard_count
    d_split = d_rows.reshape(slots, dp_count, out_width).transpose(1, 0, 2)
    inner_rows = -(-slots // out_width)
    pad_rows = (-(slots + inner_rows)) % 16
    inner_block = jnp.pad(inner, (0, inner_rows * out_width - slots)).reshape(1, inner_rows, out_width)
    extra = jnp.concatenate(
        [inner_block, jnp.zeros((1, pad_rows, out_width), jnp.bfloat16)], axis=1
    )
    extra = jnp.broadcast_to(extra, (dp_count,) + extra.shape[1:])
    ex_send = jnp.concatenate([d_split, extra], axis=1)
    ex_recv = lax.all_to_all(ex_send, ("l", "sy", "sx", "c"), split_axis=0, concat_axis=0, tiled=True)
    ex_recv = ex_recv.reshape((group_size, shard_count) + ex_recv.shape[1:])
    summed = jnp.sum(ex_recv.astype(jnp.float32), axis=1)
    grads_chunk = summed[:, :slots].reshape(group_size, dest_count, send_rows, out_width)
    grads_chunk = grads_chunk.transpose(1, 0, 2, 3).astype(jnp.bfloat16)
    inner_sum = summed[:, slots:slots + inner_rows].reshape(group_size, inner_rows * out_width)
    inner_sum = inner_sum[:, :slots].reshape(group_size, dest_count, send_rows).transpose(1, 0, 2)
    inner_hi = inner_sum.astype(jnp.bfloat16)
    inner_lo = (inner_sum - inner_hi.astype(jnp.float32)).astype(jnp.bfloat16)
    inner_pair = jnp.concatenate([inner_hi, inner_lo], axis=2).reshape(dest_count, group_size, 1, 2 * send_rows)
    inner_pair = jnp.pad(inner_pair, ((0, 0), (0, 0), (0, 0), (0, out_width - 2 * send_rows)))
    back_send = jnp.concatenate([grads_chunk, inner_pair], axis=2)
    back = lax.all_to_all(back_send, "expert", split_axis=0, concat_axis=0, tiled=True)

    back = back.transpose(1, 0, 2, 3)
    grads_back = back[:, :, :send_rows, :].reshape(group_size * slots, out_width)
    inner_back = back[:, :, send_rows, :2 * send_rows]
    inner_hi = inner_back[:, :, :send_rows].reshape(group_size * slots)
    inner_lo = inner_back[:, :, send_rows:].reshape(group_size * slots)
    contract_rows = (((0,), (0,)), ((), ()))
    d_tokens = lax.dot_general(
        by_token_all, grads_back, contract_rows, preferred_element_type=jnp.float32
    ).astype(jnp.bfloat16)
    d_probs = lax.dot_general(
        placing_all, inner_hi, contract_rows, preferred_element_type=jnp.float32
    ) + lax.dot_general(placing_all, inner_lo, contract_rows, preferred_element_type=jnp.float32)
    d_probs = d_probs.reshape(tok_rows, TOP)
    return (d_tokens, d_probs)


def solution(mesh):
    names = mesh.axis_names
    devices = mesh.devices
    if names != ("dp", "expert"):
        devices = devices.transpose([names.index("dp"), names.index("expert")])
    dp_size = devices.shape[0]
    split = Mesh(
        devices.reshape(GROUP, 2, dp_size // (4 * GROUP), 2, devices.shape[1]), ("l", "sy", "sx", "c", "expert")
    )
    return jax.shard_map(
        shards,
        mesh=split,
        in_specs=(
            P("expert", None),
            P("expert", None),
            P("expert", None),
            P("expert", None),
            P("expert", ("l", "sy", "sx", "c"), None),
            P("expert", ("l", "sy", "sx", "c"), None),
            P("expert", ("l", "sy", "sx", "c"), None),
        ),
        out_specs=(P("expert", ("l", "sy", "sx", "c")), P("expert", None)),
        check_vma=False,
    )
```

```python
import jax
import jax.numpy as jnp
from jax import lax
from jax.sharding import Mesh
from jax.sharding import PartitionSpec as P

FF = 1536
TOP = 8
GROUP = 2


def slot_tables(expert_ids, shard_type, group_size, dest_count, send_rows):
    tok_rows, top_count = expert_ids.shape
    flat_ids = expert_ids.reshape(-1)
    chosen = flat_ids % group_size == shard_type
    target = flat_ids // group_size
    columns = lax.broadcasted_iota(jnp.int32, (flat_ids.shape[0], dest_count), 1)
    matched = jnp.logical_and(chosen[:, None], target[:, None] == columns).astype(jnp.int32)
    ranking = jnp.sum((jnp.cumsum(matched, axis=0) - 1) * matched, axis=1)
    row_index = jnp.where(chosen, target * send_rows + ranking, -1)
    rows_iota = lax.broadcasted_iota(jnp.int32, (dest_count * send_rows, flat_ids.shape[0]), 0)
    placing = (rows_iota == row_index[None, :]).astype(jnp.bfloat16)
    by_token = placing.reshape(dest_count * send_rows, tok_rows, top_count).sum(axis=2)
    return (placing, by_token)


def shards(tokens, cotangent, expert_ids, gate_probs, w_gate, w_up, w_down):
    dest_count = lax.axis_size("expert")
    shard_width = w_gate.shape[1]
    shard_count = FF // shard_width
    group_size = lax.axis_size("l")
    shard_type = lax.axis_index("l")
    part = (lax.axis_index("sy") * lax.axis_size("sx") + lax.axis_index("sx")) * lax.axis_size("c") + lax.axis_index("c")
    core = lax.axis_index("c")
    tok_rows = tokens.shape[0]
    model_width = tokens.shape[1]
    chunk = model_width // shard_count
    out_width = chunk // group_size
    experts_all = group_size * dest_count
    send_rows = (4 * tok_rows * TOP + 3 * experts_all - 1) // (3 * experts_all)
    slots = dest_count * send_rows
    tables = [slot_tables(expert_ids, kind, group_size, dest_count, send_rows) for kind in range(group_size)]
    placing_all = jnp.concatenate([t[0] for t in tables], axis=0)
    by_token_all = jnp.concatenate([t[1] for t in tables], axis=0)
    placing = lax.dynamic_slice_in_dim(placing_all, shard_type * slots, slots, axis=0)
    by_token = lax.dynamic_slice_in_dim(by_token_all, shard_type * slots, slots, axis=0)

    tok_chunk = lax.dynamic_slice_in_dim(tokens, part * chunk, chunk, axis=1)
    cot_chunk = lax.dynamic_slice_in_dim(cotangent, part * chunk, chunk, axis=1)
    both_chunk = jnp.concatenate([tok_chunk, cot_chunk], axis=1)
    rows_sent = jnp.dot(by_token, both_chunk, preferred_element_type=jnp.float32).astype(jnp.bfloat16)
    rows_sent = rows_sent.reshape(dest_count, send_rows, 2 * chunk)
    probs_sent = jnp.dot(
        placing, gate_probs.reshape(-1), preferred_element_type=jnp.float32
    ).astype(jnp.bfloat16)
    probs_row = jnp.pad(probs_sent.reshape(dest_count, 1, send_rows), ((0, 0), (0, 0), (0, 2 * chunk - send_rows)))
    payload = jnp.concatenate([rows_sent, probs_row], axis=1)
    recv = lax.all_to_all(payload, "expert", split_axis=0, concat_axis=0, tiled=True)
    probs_in = recv[:, send_rows, :send_rows].reshape(slots).astype(jnp.float32)
    rows_in = recv[:, :send_rows, :].reshape(slots, 2 * chunk)

    chips = lax.axis_size("sy") * lax.axis_size("sx")
    spread = jnp.broadcast_to(rows_in[None], (chips,) + rows_in.shape)
    same_core = lax.all_to_all(spread, ("sy", "sx"), split_axis=0, concat_axis=0, tiled=True)
    other_core = lax.ppermute(same_core, "c", perm=[(0, 1), (1, 0)])
    by_core = jnp.stack([same_core, other_core, same_core], axis=1)
    gathered = lax.dynamic_slice_in_dim(by_core, core, 2, axis=1).reshape((shard_count,) + rows_in.shape)
    tok_parts = gathered[:, :, :chunk]
    cot_parts = gathered[:, :, chunk:]
    gate_shard = w_gate[0]
    up_shard = w_up[0]
    down_shard = w_down[0]
    contract_parts = (((0, 2), (1, 2)), ((), ()))

    def by_parts(weight):
        return weight.reshape(weight.shape[0], shard_count, chunk)

    pre_gate = lax.dot_general(tok_parts, by_parts(gate_shard), contract_parts, preferred_element_type=jnp.float32)
    pre_up = lax.dot_general(tok_parts, by_parts(up_shard), contract_parts, preferred_element_type=jnp.float32)
    sigmoid_gate = jax.nn.sigmoid(pre_gate)
    activated = pre_gate * sigmoid_gate
    hidden = (activated * pre_up).astype(jnp.bfloat16)
    outputs = jnp.dot(hidden, down_shard, preferred_element_type=jnp.float32).astype(jnp.bfloat16)
    outputs = lax.optimization_barrier(outputs)
    out_parts = outputs.reshape(slots, shard_count, chunk).transpose(1, 0, 2)
    inner = jnp.sum(
        cot_parts.astype(jnp.float32) * out_parts.astype(jnp.float32), axis=(0, 2)
    ).astype(jnp.bfloat16)
    d_hidden = lax.dot_general(cot_parts, by_parts(down_shard), contract_parts, preferred_element_type=jnp.float32)
    d_hidden = d_hidden * probs_in.reshape(-1, 1)
    d_up = (d_hidden * activated).astype(jnp.bfloat16)
    d_gate = (d_hidden * pre_up * sigmoid_gate * (1.0 + pre_gate * (1.0 - sigmoid_gate))).astype(
        jnp.bfloat16
    )
    d_rows = jnp.dot(d_gate, gate_shard, preferred_element_type=jnp.float32) + jnp.dot(
        d_up, up_shard, preferred_element_type=jnp.float32
    )
    d_rows = d_rows.astype(jnp.bfloat16)
    dp_count = group_size * shard_count
    d_split = d_rows.reshape(slots, dp_count, out_width).transpose(1, 0, 2)
    inner_rows = -(-slots // out_width)
    pad_rows = (-(slots + inner_rows)) % 16
    inner_block = jnp.pad(inner, (0, inner_rows * out_width - slots)).reshape(1, inner_rows, out_width)
    extra = jnp.concatenate(
        [inner_block, jnp.zeros((1, pad_rows, out_width), jnp.bfloat16)], axis=1
    )
    extra = jnp.broadcast_to(extra, (dp_count,) + extra.shape[1:])
    ex_send = jnp.concatenate([d_split, extra], axis=1)
    ex_recv = lax.all_to_all(ex_send, ("l", "sy", "sx", "c"), split_axis=0, concat_axis=0, tiled=True)
    ex_recv = ex_recv.reshape((group_size, shard_count) + ex_recv.shape[1:])
    summed = jnp.sum(ex_recv.astype(jnp.float32), axis=1)
    grads_chunk = summed[:, :slots].reshape(group_size, dest_count, send_rows, out_width)
    grads_chunk = grads_chunk.transpose(1, 0, 2, 3).astype(jnp.bfloat16)
    inner_sum = summed[:, slots:slots + inner_rows].reshape(group_size, inner_rows * out_width)
    inner_sum = inner_sum[:, :slots].reshape(group_size, dest_count, send_rows).transpose(1, 0, 2)
    inner_hi = inner_sum.astype(jnp.bfloat16)
    inner_lo = (inner_sum - inner_hi.astype(jnp.float32)).astype(jnp.bfloat16)
    inner_pair = jnp.concatenate([inner_hi, inner_lo], axis=2).reshape(dest_count, group_size, 1, 2 * send_rows)
    inner_pair = jnp.pad(inner_pair, ((0, 0), (0, 0), (0, 0), (0, out_width - 2 * send_rows)))
    back_send = jnp.concatenate([grads_chunk, inner_pair], axis=2)
    back = lax.all_to_all(back_send, "expert", split_axis=0, concat_axis=0, tiled=True)

    back = back.transpose(1, 0, 2, 3)
    grads_back = back[:, :, :send_rows, :].reshape(group_size * slots, out_width)
    inner_back = back[:, :, send_rows, :2 * send_rows]
    inner_hi = inner_back[:, :, :send_rows].reshape(group_size * slots)
    inner_lo = inner_back[:, :, send_rows:].reshape(group_size * slots)
    contract_rows = (((0,), (0,)), ((), ()))
    d_tokens = lax.dot_general(
        by_token_all, grads_back, contract_rows, preferred_element_type=jnp.float32
    ).astype(jnp.bfloat16)
    d_probs = lax.dot_general(
        placing_all, inner_hi, contract_rows, preferred_element_type=jnp.float32
    ) + lax.dot_general(placing_all, inner_lo, contract_rows, preferred_element_type=jnp.float32)
    d_probs = d_probs.reshape(tok_rows, TOP)
    return (d_tokens, d_probs)


def solution(mesh):
    names = mesh.axis_names
    devices = mesh.devices
    if names != ("dp", "expert"):
        devices = devices.transpose([names.index("dp"), names.index("expert")])
    dp_size = devices.shape[0]
    split = Mesh(
        devices.reshape(GROUP, 2, dp_size // (4 * GROUP), 2, devices.shape[1]), ("l", "sy", "sx", "c", "expert")
    )
    return jax.shard_map(
        shards,
        mesh=split,
        in_specs=(
            P("expert", None),
            P("expert", None),
            P("expert", None),
            P("expert", None),
            P("expert", ("l", "sy", "sx", "c"), None),
            P("expert", ("l", "sy", "sx", "c"), None),
            P("expert", ("l", "sy", "sx", "c"), None),
        ),
        out_specs=(P("expert", ("l", "sy", "sx", "c")), P("expert", None)),
        check_vma=False,
    )
```

```python
import jax
import jax.numpy as jnp
from jax import lax
from jax.sharding import Mesh
from jax.sharding import PartitionSpec as P

FF = 1536
TOP = 8
GROUP = 2


def slot_tables(expert_ids, shard_type, group_size, dest_count, send_rows):
    tok_rows, top_count = expert_ids.shape
    flat_ids = expert_ids.reshape(-1)
    chosen = flat_ids % group_size == shard_type
    target = flat_ids // group_size
    columns = lax.broadcasted_iota(jnp.int32, (flat_ids.shape[0], dest_count), 1)
    matched = jnp.logical_and(chosen[:, None], target[:, None] == columns).astype(jnp.int32)
    ranking = jnp.sum((jnp.cumsum(matched, axis=0) - 1) * matched, axis=1)
    row_index = jnp.where(chosen, target * send_rows + ranking, -1)
    rows_iota = lax.broadcasted_iota(jnp.int32, (dest_count * send_rows, flat_ids.shape[0]), 0)
    placing = (rows_iota == row_index[None, :]).astype(jnp.bfloat16)
    by_token = placing.reshape(dest_count * send_rows, tok_rows, top_count).sum(axis=2)
    return (placing, by_token)


def shards(tokens, cotangent, expert_ids, gate_probs, w_gate, w_up, w_down):
    dest_count = lax.axis_size("expert")
    shard_width = w_gate.shape[1]
    shard_count = FF // shard_width
    group_size = lax.axis_size("l")
    shard_type = lax.axis_index("l")
    part = (lax.axis_index("sy") * lax.axis_size("sx") + lax.axis_index("sx")) * lax.axis_size("c") + lax.axis_index("c")
    core = lax.axis_index("c")
    tok_rows = tokens.shape[0]
    model_width = tokens.shape[1]
    chunk = model_width // shard_count
    out_width = chunk // group_size
    experts_all = group_size * dest_count
    send_rows = (4 * tok_rows * TOP + 3 * experts_all - 1) // (3 * experts_all)
    slots = dest_count * send_rows
    tables = [slot_tables(expert_ids, kind, group_size, dest_count, send_rows) for kind in range(group_size)]
    placing_all = jnp.concatenate([t[0] for t in tables], axis=0)
    by_token_all = jnp.concatenate([t[1] for t in tables], axis=0)
    placing = lax.dynamic_slice_in_dim(placing_all, shard_type * slots, slots, axis=0)
    by_token = lax.dynamic_slice_in_dim(by_token_all, shard_type * slots, slots, axis=0)

    tok_chunk = lax.dynamic_slice_in_dim(tokens, part * chunk, chunk, axis=1)
    cot_chunk = lax.dynamic_slice_in_dim(cotangent, part * chunk, chunk, axis=1)
    both_chunk = jnp.concatenate([tok_chunk, cot_chunk], axis=1)
    rows_sent = jnp.dot(by_token, both_chunk, preferred_element_type=jnp.float32).astype(jnp.bfloat16)
    rows_sent = rows_sent.reshape(dest_count, send_rows, 2 * chunk)
    probs_sent = jnp.dot(
        placing, gate_probs.reshape(-1), preferred_element_type=jnp.float32
    ).astype(jnp.bfloat16)
    probs_row = jnp.pad(probs_sent.reshape(dest_count, 1, send_rows), ((0, 0), (0, 0), (0, 2 * chunk - send_rows)))
    payload = jnp.concatenate([rows_sent, probs_row], axis=1)
    recv = lax.all_to_all(payload, "expert", split_axis=0, concat_axis=0, tiled=True)
    probs_in = recv[:, send_rows, :send_rows].reshape(slots).astype(jnp.float32)
    rows_in = recv[:, :send_rows, :].reshape(slots, 2 * chunk)

    chips = lax.axis_size("sy") * lax.axis_size("sx")
    spread = jnp.broadcast_to(rows_in[None], (chips,) + rows_in.shape)
    same_core = lax.all_to_all(spread, ("sy", "sx"), split_axis=0, concat_axis=0, tiled=True)
    other_core = lax.ppermute(same_core, "c", perm=[(0, 1), (1, 0)])
    by_core = jnp.stack([same_core, other_core, same_core], axis=1)
    gathered = lax.dynamic_slice_in_dim(by_core, core, 2, axis=1).reshape((shard_count,) + rows_in.shape)
    tok_parts = gathered[:, :, :chunk]
    cot_parts = gathered[:, :, chunk:]
    rows_tok = tok_parts.transpose(1, 0, 2).reshape(slots, model_width)
    rows_cot = cot_parts.transpose(1, 0, 2).reshape(slots, model_width)
    gate_shard = w_gate[0]
    up_shard = w_up[0]
    down_shard = w_down[0]
    contract_model = (((1,), (1,)), ((), ()))
    pre_gate = lax.dot_general(rows_tok, gate_shard, contract_model, preferred_element_type=jnp.float32)
    pre_up = lax.dot_general(rows_tok, up_shard, contract_model, preferred_element_type=jnp.float32)
    sigmoid_gate = jax.nn.sigmoid(pre_gate)
    activated = pre_gate * sigmoid_gate
    hidden = (activated * pre_up).astype(jnp.bfloat16)
    outputs = jnp.dot(hidden, down_shard, preferred_element_type=jnp.float32).astype(jnp.bfloat16)
    inner = jnp.sum(
        rows_cot.astype(jnp.float32) * outputs.astype(jnp.float32), axis=1
    ).astype(jnp.bfloat16)
    d_hidden = lax.dot_general(rows_cot, down_shard, contract_model, preferred_element_type=jnp.float32)
    d_hidden = d_hidden * probs_in.reshape(-1, 1)
    d_up = (d_hidden * activated).astype(jnp.bfloat16)
    d_gate = (d_hidden * pre_up * sigmoid_gate * (1.0 + pre_gate * (1.0 - sigmoid_gate))).astype(
        jnp.bfloat16
    )
    d_rows = jnp.dot(d_gate, gate_shard, preferred_element_type=jnp.float32) + jnp.dot(
        d_up, up_shard, preferred_element_type=jnp.float32
    )
    d_rows = d_rows.astype(jnp.bfloat16)
    dp_count = group_size * shard_count
    d_split = d_rows.reshape(slots, dp_count, out_width).transpose(1, 0, 2)
    inner_rows = -(-slots // out_width)
    pad_rows = (-(slots + inner_rows)) % 16
    inner_block = jnp.pad(inner, (0, inner_rows * out_width - slots)).reshape(1, inner_rows, out_width)
    extra = jnp.concatenate(
        [inner_block, jnp.zeros((1, pad_rows, out_width), jnp.bfloat16)], axis=1
    )
    extra = jnp.broadcast_to(extra, (dp_count,) + extra.shape[1:])
    ex_send = jnp.concatenate([d_split, extra], axis=1)
    ex_recv = lax.all_to_all(ex_send, ("l", "sy", "sx", "c"), split_axis=0, concat_axis=0, tiled=True)
    ex_recv = ex_recv.reshape((group_size, shard_count) + ex_recv.shape[1:])
    summed = jnp.sum(ex_recv.astype(jnp.float32), axis=1)
    grads_chunk = summed[:, :slots].reshape(group_size, dest_count, send_rows, out_width)
    grads_chunk = grads_chunk.transpose(1, 0, 2, 3).astype(jnp.bfloat16)
    inner_sum = summed[:, slots:slots + inner_rows].reshape(group_size, inner_rows * out_width)
    inner_sum = inner_sum[:, :slots].reshape(group_size, dest_count, send_rows).transpose(1, 0, 2)
    inner_hi = inner_sum.astype(jnp.bfloat16)
    inner_lo = (inner_sum - inner_hi.astype(jnp.float32)).astype(jnp.bfloat16)
    inner_pair = jnp.concatenate([inner_hi, inner_lo], axis=2).reshape(dest_count, group_size, 1, 2 * send_rows)
    inner_pair = jnp.pad(inner_pair, ((0, 0), (0, 0), (0, 0), (0, out_width - 2 * send_rows)))
    back_send = jnp.concatenate([grads_chunk, inner_pair], axis=2)
    back = lax.all_to_all(back_send, "expert", split_axis=0, concat_axis=0, tiled=True)

    back = back.transpose(1, 0, 2, 3)
    grads_back = back[:, :, :send_rows, :].reshape(group_size * slots, out_width)
    inner_back = back[:, :, send_rows, :2 * send_rows]
    inner_hi = inner_back[:, :, :send_rows].reshape(group_size * slots)
    inner_lo = inner_back[:, :, send_rows:].reshape(group_size * slots)
    contract_rows = (((0,), (0,)), ((), ()))
    d_tokens = lax.dot_general(
        by_token_all, grads_back, contract_rows, preferred_element_type=jnp.float32
    ).astype(jnp.bfloat16)
    d_probs = lax.dot_general(
        placing_all, inner_hi, contract_rows, preferred_element_type=jnp.float32
    ) + lax.dot_general(placing_all, inner_lo, contract_rows, preferred_element_type=jnp.float32)
    d_probs = d_probs.reshape(tok_rows, TOP)
    return (d_tokens, d_probs)


def solution(mesh):
    names = mesh.axis_names
    devices = mesh.devices
    if names != ("dp", "expert"):
        devices = devices.transpose([names.index("dp"), names.index("expert")])
    dp_size = devices.shape[0]
    split = Mesh(
        devices.reshape(GROUP, 2, dp_size // (4 * GROUP), 2, devices.shape[1]), ("l", "sy", "sx", "c", "expert")
    )
    return jax.shard_map(
        shards,
        mesh=split,
        in_specs=(
            P("expert", None),
            P("expert", None),
            P("expert", None),
            P("expert", None),
            P("expert", ("l", "sy", "sx", "c"), None),
            P("expert", ("l", "sy", "sx", "c"), None),
            P("expert", ("l", "sy", "sx", "c"), None),
        ),
        out_specs=(P("expert", ("l", "sy", "sx", "c")), P("expert", None)),
        check_vma=False,
    )
```
